128 devices in a mesh: seq: 32 (over z, x, core), tp: 4 (over y).
Axes of the slice: x: 4, y: 4, z: 4, core: 2. Of those that a mesh axis runs over, the one named last changes fastest.
Arguments:
- streams: bfloat16 [3, 16384, 2048], P(None, 'seq', 'tp'), may hold values from -6 to 6
- short_taps: float32 [3, 3, 2048], P(None, None, 'tp'), may hold values from -3 to 3
- filter_taps: float32 [16384, 2048], P('seq', 'tp'), may hold values from -0.046875 to 0.046875
- skip_gain: float32 [2048], P('tp'), may hold values from -4 to 4
- w_out: bfloat16 [2048, 4096], P('tp'), may hold values from -0.1875 to 0.1875
- cotangent: bfloat16 [16384, 4096], P('seq'), may hold values from -6 to 6
Outputs:
- mixed: bfloat16 [16384, 4096], P('seq', 'tp')
- stream_grads: bfloat16 [3, 16384, 2048], P(None, 'seq', 'tp')
The draws below stay inside these ranges and needn't reach their ends.
All inputs are finite; a program needn't handle non-finite values.
Results may differ from the reference program's by a relative error of at most 0.005.
Values may be sent and summed in bfloat16 or wider, within the bound.
No kernel may reach another device: no remote copies, remote signals or barrier semaphores. Data moves between devices by JAX's collectives and lax.ppermute only.
A program may use at most 128 MiB of HBM per device.

```python
import jax
import jax.numpy as jnp

D = 4096
C = 2048
L = 16384


def raised(result, stream_key, source, target, shards_of, factor):
    def block_of(position):
        return (jnp.arange(result.shape[position]) // (result.shape[position] // shards_of)).reshape((-1,) + (1,) * (result.ndim - 1 - position))

    one_side = jax.random.permutation(stream_key, shards_of)[block_of(target)]
    second = (block_of(target) + shards_of // 2) % shards_of
    return jnp.where((block_of(source) == one_side) | (block_of(source) == second), factor * result, result)


def block_levels(rng, dims, split, least, largest):
    level, own = 1.0, jax.random.fold_in(rng, 6)
    for dim, shards_of in split:
        draws = jnp.exp(jax.random.uniform(jax.random.fold_in(own, dim), (shards_of,), jnp.float32, least / len(split), largest / len(split)))
        level = level * jnp.repeat(draws, dims[dim] // shards_of).reshape([-1 if axis == dim else 1 for axis in range(len(dims))])
    return level


def normal_values(key, dims, deviation, most, cuts=(), kind=jnp.bfloat16):
    factor_of = block_levels(key, dims, cuts, -0.22, 0.18) if cuts else 1.0
    array = jax.random.normal(key, dims, jnp.float32) * deviation * factor_of
    return jnp.minimum(jnp.maximum(array, -most), most).astype(kind)


def heavy_noise(key, extent, scale, reach, cuts, heavy, kind=jnp.bfloat16):
    drawn = scale * jax.random.normal(key, extent, jnp.float32)
    if cuts:
        drawn = drawn * block_levels(key, extent, cuts, -0.22, 0.18)
    return jnp.clip(raised(drawn, jax.random.fold_in(key, 3), *heavy), -reach, reach).astype(kind)


def setup_inputs(seed: int = 0) -> dict:
    keys = jax.random.split(jax.random.key(seed), 7)
    return {
        "streams": normal_values(keys[0], (3, L, C), 1.0, 6.0, ((1, 32), (2, 4))),
        "short_taps": normal_values(keys[1], (3, 3, C), 0.6, 3.0, ((2, 4),), jnp.float32),
        "filter_taps": normal_values(keys[2], (L, C), L ** -0.5, 0.046875, ((0, 32), (1, 4)), jnp.float32),
        "skip_gain": normal_values(keys[3], (C,), 1.0, 4.0, ((0, 4),), jnp.float32),
        "w_out": heavy_noise(keys[4], (C, D), C ** -0.5, 0.1875, ((0, 4),), (0, 1, 4, 2.0)),
        "cotangent": normal_values(keys[5], (L, D), 1.0, 6.0, ((0, 32),)),
    }


def causal_taps(stream, taps):
    padded = jnp.pad(stream, ((2, 0), (0, 0)))
    return taps[0] * padded[2:] + taps[1] * padded[1:-1] + taps[2] * padded[:-2]


def ahead_taps(gradient, taps):
    padded = jnp.pad(gradient, ((0, 2), (0, 0)))
    return taps[0] * padded[:-2] + taps[1] * padded[1:-1] + taps[2] * padded[2:]


def reference(streams, short_taps, filter_taps, skip_gain, w_out, cotangent):
    length = streams.shape[1]
    points = 2 * length
    values = streams.astype(jnp.float32)
    conv_q = causal_taps(values[0], short_taps[0])
    conv_k = causal_taps(values[1], short_taps[1])
    conv_v = causal_taps(values[2], short_taps[2])
    source = conv_k * conv_v
    kernel = jnp.fft.rfft(filter_taps, n=points, axis=0)
    long_part = jnp.fft.irfft(kernel * jnp.fft.rfft(source, n=points, axis=0), n=points, axis=0)[:length]
    mixer_state = long_part + skip_gain * source
    gated = (conv_q * mixer_state).astype(jnp.bfloat16)
    mixed = jnp.dot(gated, w_out, preferred_element_type=jnp.float32).astype(jnp.bfloat16)
    grad_gated = jnp.dot(cotangent, w_out.T, preferred_element_type=jnp.float32)
    grad_q = grad_gated * mixer_state
    grad_state = grad_gated * conv_q
    grad_long = jnp.fft.irfft(jnp.conj(kernel) * jnp.fft.rfft(grad_state, n=points, axis=0), n=points, axis=0)[:length]
    grad_source = grad_long + skip_gain * grad_state
    grad_k = grad_source * conv_v
    grad_v = grad_source * conv_k
    stream_grads = jnp.stack([
        ahead_taps(grad_q, short_taps[0]),
        ahead_taps(grad_k, short_taps[1]),
        ahead_taps(grad_v, short_taps[2]),
    ]).astype(jnp.bfloat16)
    return mixed, stream_grads
```

```python
import math

import jax
import jax.numpy as jnp
from jax import lax
from jax.sharding import PartitionSpec as P

full_turn = 2.0 * math.pi
fast = lax.Precision.HIGH


def passed_along(x, axis, by):
    devices = lax.axis_size(axis)
    pairs = [(i, i + by) for i in range(devices) if 0 <= i + by < devices]
    return lax.ppermute(x, axis, pairs)


def angle_table(rows, cols, period):
    row_ids = jnp.arange(rows, dtype=jnp.int32)[:, None]
    col_ids = jnp.arange(cols, dtype=jnp.int32)[None, :]
    angles = (row_ids * col_ids % period).astype(jnp.float32) * (full_turn / period)
    return (jnp.cos(angles), jnp.sin(angles))


def forward_spectra(lanes, total):
    count = lanes.shape[2]
    length = lanes.shape[1]
    half = count + 1
    cosine, sine = angle_table(half, count, 2 * count)
    first = jnp.einsum("rkm,simc->rsikc", jnp.stack([cosine, -sine]), lanes, precision=fast)
    twist_cos, twist_sin = angle_table(length, half, total)
    twist_cos = twist_cos[:, :, None]
    twist_sin = twist_sin[:, :, None]
    real_part = first[0] * twist_cos + first[1] * twist_sin
    imag_part = first[1] * twist_cos - first[0] * twist_sin
    cos_b, sin_b = angle_table(length, length, length)
    table = jnp.stack([jnp.stack([cos_b, sin_b]), jnp.stack([-sin_b, cos_b])])
    return jnp.einsum(
        "rqji,qsikc->rsjkc", table, jnp.stack([real_part, imag_part]), precision=fast
    )


def inverse_signals(spectral, count, total):
    length = spectral.shape[2]
    half = spectral.shape[3]
    cos_b, sin_b = angle_table(length, length, length)
    table = jnp.stack([jnp.stack([cos_b, -sin_b]), jnp.stack([sin_b, cos_b])])
    block = jnp.einsum("rqij,qsjkc->rsikc", table, spectral, precision=fast)
    twist_cos, twist_sin = angle_table(length, half, total)
    twist_cos = twist_cos[:, :, None]
    twist_sin = twist_sin[:, :, None]
    real_part = block[0] * twist_cos - block[1] * twist_sin
    imag_part = block[0] * twist_sin + block[1] * twist_cos
    cosine, sine = angle_table(count, half, 2 * count)
    k_ids = jnp.arange(half, dtype=jnp.int32)[None, :]
    weight = jnp.where((k_ids == 0) | (k_ids == count), 1.0, 2.0) * (1.0 / total)
    last = jnp.stack([cosine * weight, -sine * weight])
    return jnp.einsum(
        "rmk,rsikc->simc", last, jnp.stack([real_part, imag_part]), precision=fast
    )


def on_device(streams, short_taps, filter_taps, skip_gain, w_out, cotangent):
    length = streams.shape[1]
    channels = streams.shape[2]
    devices = lax.axis_size("seq")
    groups = lax.axis_size("tp")
    total = 2 * length * devices
    lane_width = channels // devices

    w_cols = lax.all_to_all(
        w_out.reshape(channels, groups, -1), "tp", split_axis=1, concat_axis=0, tiled=True
    )[:, 0]

    previous = passed_along(streams[:, -2:, :], "seq", 1)
    extended = jnp.concatenate([previous, streams], axis=1).astype(jnp.float32)
    convolved = (
        short_taps[:, 0, None, :] * extended[:, 2:]
        + short_taps[:, 1, None, :] * extended[:, 1:-1]
        + short_taps[:, 2, None, :] * extended[:, :-2]
    )
    conv_q = convolved[0]
    conv_k = convolved[1]
    conv_v = convolved[2]
    source = conv_k * conv_v
    grad_gated = lax.dot_general(
        cotangent, w_out, (((1,), (1,)), ((), ())), preferred_element_type=jnp.float32
    )
    grad_state = grad_gated * conv_q

    signals = jnp.stack([source, filter_taps, grad_state]).reshape(3, length, devices, lane_width)
    lanes = lax.all_to_all(signals, "seq", split_axis=2, concat_axis=2, tiled=True)
    spectra = forward_spectra(lanes, total)
    data_real = spectra[0, 0]
    data_imag = spectra[1, 0]
    kernel_real = spectra[0, 1]
    kernel_imag = spectra[1, 1]
    grad_real = spectra[0, 2]
    grad_imag = spectra[1, 2]
    products = jnp.stack(
        [
            jnp.stack(
                [
                    data_real * kernel_real - data_imag * kernel_imag,
                    grad_real * kernel_real + grad_imag * kernel_imag,
                ]
            ),
            jnp.stack(
                [
                    data_real * kernel_imag + data_imag * kernel_real,
                    grad_imag * kernel_real - grad_real * kernel_imag,
                ]
            ),
        ]
    )
    back = inverse_signals(products, devices, total)
    restored = lax.all_to_all(back, "seq", split_axis=2, concat_axis=2, tiled=True)
    restored = restored.reshape(2, length, channels)

    mixer_state = restored[0] + skip_gain * source
    gated = (conv_q * mixer_state).astype(jnp.bfloat16)
    gated_all = lax.all_gather(gated, "tp", axis=1, tiled=True)
    mixed = jnp.dot(gated_all, w_cols, preferred_element_type=jnp.float32).astype(jnp.bfloat16)

    grad_q = grad_gated * mixer_state
    grad_source = restored[1] + skip_gain * grad_state
    gradients = jnp.stack([grad_q, grad_source * conv_v, grad_source * conv_k])
    following = passed_along(gradients[:, :2, :], "seq", -1)
    grad_ext = jnp.concatenate([gradients, following], axis=1)
    stream_grads = (
        short_taps[:, 0, None, :] * grad_ext[:, :-2]
        + short_taps[:, 1, None, :] * grad_ext[:, 1:-1]
        + short_taps[:, 2, None, :] * grad_ext[:, 2:]
    )
    return (mixed, stream_grads.astype(jnp.bfloat16))


def solution(mesh):
    return jax.shard_map(
        on_device,
        mesh=mesh,
        in_specs=(
            P(None, "seq", "tp"),
            P(None, None, "tp"),
            P("seq", "tp"),
            P("tp"),
            P("tp", None),
            P("seq", None),
        ),
        out_specs=(P("seq", "tp"), P(None, "seq", "tp")),
        check_vma=False,
    )
```

```python
import math

import jax
import jax.numpy as jnp
from jax import lax
from jax.sharding import PartitionSpec as P

full_turn = 2.0 * math.pi
fast = lax.Precision.HIGH


def passed_along(x, axis, by):
    devices = lax.axis_size(axis)
    pairs = [(i, i + by) for i in range(devices) if 0 <= i + by < devices]
    return lax.ppermute(x, axis, pairs)


def angle_table(rows, cols, period):
    row_ids = jnp.arange(rows, dtype=jnp.int32)[:, None]
    col_ids = jnp.arange(cols, dtype=jnp.int32)[None, :]
    angles = (row_ids * col_ids % period).astype(jnp.float32) * (full_turn / period)
    return (jnp.cos(angles), jnp.sin(angles))


def forward_spectra(lanes, total):
    count = lanes.shape[2]
    length = lanes.shape[1]
    half = count + 1
    cosine, sine = angle_table(half, count, 2 * count)
    first = jnp.einsum("rkm,simc->rsikc", jnp.stack([cosine, -sine]), lanes, precision=fast)
    twist_cos, twist_sin = angle_table(length, half, total)
    twist_cos = twist_cos[:, :, None]
    twist_sin = twist_sin[:, :, None]
    real_part = first[0] * twist_cos + first[1] * twist_sin
    imag_part = first[1] * twist_cos - first[0] * twist_sin
    cos_b, sin_b = angle_table(length, length, length)
    table = jnp.stack([jnp.stack([cos_b, sin_b]), jnp.stack([-sin_b, cos_b])])
    return jnp.einsum(
        "rqji,qsikc->rsjkc", table, jnp.stack([real_part, imag_part]), precision=fast
    )


def inverse_signals(spectral, count, total):
    length = spectral.shape[2]
    half = spectral.shape[3]
    cos_b, sin_b = angle_table(length, length, length)
    table = jnp.stack([jnp.stack([cos_b, -sin_b]), jnp.stack([sin_b, cos_b])])
    block = jnp.einsum("rqij,qsjkc->rsikc", table, spectral, precision=fast)
    twist_cos, twist_sin = angle_table(length, half, total)
    twist_cos = twist_cos[:, :, None]
    twist_sin = twist_sin[:, :, None]
    real_part = block[0] * twist_cos - block[1] * twist_sin
    imag_part = block[0] * twist_sin + block[1] * twist_cos
    cosine, sine = angle_table(count, half, 2 * count)
    k_ids = jnp.arange(half, dtype=jnp.int32)[None, :]
    weight = jnp.where((k_ids == 0) | (k_ids == count), 1.0, 2.0) * (1.0 / total)
    last = jnp.stack([cosine * weight, -sine * weight])
    return jnp.einsum(
        "rmk,rsikc->simc", last, jnp.stack([real_part, imag_part]), precision=fast
    )


def spectra_products(filter_spectra, spectra):
    kernel_real = filter_spectra[0, 0]
    kernel_imag = filter_spectra[1, 0]
    data_real = spectra[0, 0]
    data_imag = spectra[1, 0]
    grad_real = spectra[0, 1]
    grad_imag = spectra[1, 1]
    return jnp.stack(
        [
            jnp.stack(
                [
                    data_real * kernel_real - data_imag * kernel_imag,
                    grad_real * kernel_real + grad_imag * kernel_imag,
                ]
            ),
            jnp.stack(
                [
                    data_real * kernel_imag + data_imag * kernel_real,
                    grad_imag * kernel_real - grad_real * kernel_imag,
                ]
            ),
        ]
    )


def on_device(streams, short_taps, filter_taps, skip_gain, w_out, cotangent):
    length = streams.shape[1]
    channels = streams.shape[2]
    devices = lax.axis_size("seq")
    groups = lax.axis_size("tp")
    total = 2 * length * devices
    lane_width = channels // devices
    features = w_out.shape[1] // groups
    me = lax.axis_index("tp")

    def exchanged(x, shift):
        return lax.ppermute(x, "tp", [(i, (i + shift) % groups) for i in range(groups)])

    core = lax.axis_index("seq") % 2
    half_width = features // 2
    own_block = lax.dynamic_slice_in_dim(w_out, me * features, features, axis=1)
    fetched = []
    for shift in range(1, groups):
        target = (me + shift) % groups
        piece = lax.dynamic_slice_in_dim(w_out, target * features + core * half_width, half_width, axis=1)
        fetched.append(exchanged(piece, shift))
    fetched = jnp.stack(fetched)
    partner = lax.ppermute(fetched, "seq", [(i, i ^ 1) for i in range(devices)])

    filter_lanes = lax.all_to_all(
        filter_taps.reshape(1, length, devices, lane_width), "seq", split_axis=2, concat_axis=2, tiled=True
    )

    previous = passed_along(streams[:, -2:, :], "seq", 1)
    extended = jnp.concatenate([previous, streams], axis=1).astype(jnp.float32)
    convolved = (
        short_taps[:, 0, None, :] * extended[:, 2:]
        + short_taps[:, 1, None, :] * extended[:, 1:-1]
        + short_taps[:, 2, None, :] * extended[:, :-2]
    )
    conv_q = convolved[0]
    conv_k = convolved[1]
    conv_v = convolved[2]
    source = conv_k * conv_v
    grad_gated = lax.dot_general(
        cotangent, w_out, (((1,), (1,)), ((), ())), preferred_element_type=jnp.float32
    )
    grad_state = grad_gated * conv_q

    signals = jnp.stack([source, grad_state]).reshape(2, length, devices, lane_width)
    lanes = lax.all_to_all(signals, "seq", split_axis=2, concat_axis=2, tiled=True)
    fetched, partner, lanes = lax.optimization_barrier((fetched, partner, lanes))
    filter_spectra = forward_spectra(filter_lanes, total)
    spectra = forward_spectra(lanes, total)
    products = spectra_products(filter_spectra, spectra)

    long_back = inverse_signals(products[:, 0:1], devices, total)
    long_part = lax.all_to_all(long_back, "seq", split_axis=2, concat_axis=2, tiled=True)
    grad_back = inverse_signals(products[:, 1:2], devices, total)

    mixer_state = long_part.reshape(length, channels) + skip_gain * source
    gated = (conv_q * mixer_state).astype(jnp.bfloat16)
    gated, grad_back = lax.optimization_barrier((gated, grad_back))
    grad_long = lax.all_to_all(grad_back, "seq", split_axis=2, concat_axis=2, tiled=True)
    mine = jnp.dot(gated, lax.dynamic_slice_in_dim(own_block, core * half_width, half_width, axis=1),
                   preferred_element_type=jnp.float32)
    other = jnp.dot(gated, lax.dynamic_slice_in_dim(own_block, (1 - core) * half_width, half_width, axis=1),
                    preferred_element_type=jnp.float32)
    for shift in range(1, groups):
        received = exchanged(gated, shift)
        mine = mine + jnp.dot(received, fetched[shift - 1], preferred_element_type=jnp.float32)
        other = other + jnp.dot(received, partner[shift - 1], preferred_element_type=jnp.float32)
    terms = jnp.where(core == 0, jnp.concatenate([mine, other], axis=1), jnp.concatenate([other, mine], axis=1))
    mixed = terms.astype(jnp.bfloat16)

    grad_q = grad_gated * mixer_state
    grad_source = grad_long.reshape(length, channels) + skip_gain * grad_state
    gradients = jnp.stack([grad_q, grad_source * conv_v, grad_source * conv_k])
    following = passed_along(gradients[:, :2, :], "seq", -1)
    grad_ext = jnp.concatenate([gradients, following], axis=1)
    stream_grads = (
        short_taps[:, 0, None, :] * grad_ext[:, :-2]
        + short_taps[:, 1, None, :] * grad_ext[:, 1:-1]
        + short_taps[:, 2, None, :] * grad_ext[:, 2:]
    )
    return (mixed, stream_grads.astype(jnp.bfloat16))


def solution(mesh):
    return jax.shard_map(
        on_device,
        mesh=mesh,
        in_specs=(
            P(None, "seq", "tp"),
            P(None, None, "tp"),
            P("seq", "tp"),
            P("tp"),
            P("tp", None),
            P("seq", None),
        ),
        out_specs=(P("seq", "tp"), P(None, "seq", "tp")),
        check_vma=False,
    )
```

```python
import math

import jax
import jax.numpy as jnp
from jax import lax
from jax.sharding import PartitionSpec as P

full_turn = 2.0 * math.pi
fast = lax.Precision.HIGH


def passed_along(x, axis, by):
    devices = lax.axis_size(axis)
    pairs = [(i, i + by) for i in range(devices) if 0 <= i + by < devices]
    return lax.ppermute(x, axis, pairs)


def angle_table(rows, cols, period):
    row_ids = jnp.arange(rows, dtype=jnp.int32)[:, None]
    col_ids = jnp.arange(cols, dtype=jnp.int32)[None, :]
    angles = (row_ids * col_ids % period).astype(jnp.float32) * (full_turn / period)
    return (jnp.cos(angles), jnp.sin(angles))


def forward_spectra(lanes, total):
    count = lanes.shape[2]
    length = lanes.shape[1]
    half = count + 1
    cosine, sine = angle_table(half, count, 2 * count)
    first = jnp.einsum("rkm,simc->rsikc", jnp.stack([cosine, -sine]), lanes, precision=fast)
    twist_cos, twist_sin = angle_table(length, half, total)
    twist_cos = twist_cos[:, :, None]
    twist_sin = twist_sin[:, :, None]
    real_part = first[0] * twist_cos + first[1] * twist_sin
    imag_part = first[1] * twist_cos - first[0] * twist_sin
    cos_b, sin_b = angle_table(length, length, length)
    table = jnp.stack([jnp.stack([cos_b, sin_b]), jnp.stack([-sin_b, cos_b])])
    return jnp.einsum(
        "rqji,qsikc->rsjkc", table, jnp.stack([real_part, imag_part]), precision=fast
    )


def inverse_signals(spectral, count, total):
    length = spectral.shape[2]
    half = spectral.shape[3]
    cos_b, sin_b = angle_table(length, length, length)
    table = jnp.stack([jnp.stack([cos_b, -sin_b]), jnp.stack([sin_b, cos_b])])
    block = jnp.einsum("rqij,qsjkc->rsikc", table, spectral, precision=fast)
    twist_cos, twist_sin = angle_table(length, half, total)
    twist_cos = twist_cos[:, :, None]
    twist_sin = twist_sin[:, :, None]
    real_part = block[0] * twist_cos - block[1] * twist_sin
    imag_part = block[0] * twist_sin + block[1] * twist_cos
    cosine, sine = angle_table(count, half, 2 * count)
    k_ids = jnp.arange(half, dtype=jnp.int32)[None, :]
    weight = jnp.where((k_ids == 0) | (k_ids == count), 1.0, 2.0) * (1.0 / total)
    last = jnp.stack([cosine * weight, -sine * weight])
    return jnp.einsum(
        "rmk,rsikc->simc", last, jnp.stack([real_part, imag_part]), precision=fast
    )


def on_device(streams, short_taps, filter_taps, skip_gain, w_out, cotangent):
    length = streams.shape[1]
    channels = streams.shape[2]
    devices = lax.axis_size("seq")
    groups = lax.axis_size("tp")
    total = 2 * length * devices
    lane_width = channels // devices
    features = w_out.shape[1] // groups
    me = lax.axis_index("tp")

    def exchanged(x, shift):
        return lax.ppermute(x, "tp", [(i, (i + shift) % groups) for i in range(groups)])

    core = lax.axis_index("seq") % 2
    half_width = features // 2
    own_block = lax.dynamic_slice_in_dim(w_out, me * features, features, axis=1)
    fetched = []
    for shift in range(1, groups):
        target = (me + shift) % groups
        piece = lax.dynamic_slice_in_dim(w_out, target * features + core * half_width, half_width, axis=1)
        fetched.append(exchanged(piece, shift))
    fetched = jnp.stack(fetched)
    partner = lax.ppermute(fetched, "seq", [(i, i ^ 1) for i in range(devices)])

    filter_lanes = lax.all_to_all(
        filter_taps.reshape(1, length, devices, lane_width), "seq", split_axis=2, concat_axis=2, tiled=True
    )

    previous = passed_along(streams[:, -2:, :], "seq", 1)
    extended = jnp.concatenate([previous, streams], axis=1).astype(jnp.float32)
    convolved = (
        short_taps[:, 0, None, :] * extended[:, 2:]
        + short_taps[:, 1, None, :] * extended[:, 1:-1]
        + short_taps[:, 2, None, :] * extended[:, :-2]
    )
    conv_q = convolved[0]
    conv_k = convolved[1]
    conv_v = convolved[2]
    source = conv_k * conv_v
    grad_gated = lax.dot_general(
        cotangent, w_out, (((1,), (1,)), ((), ())), preferred_element_type=jnp.float32
    )
    grad_state = grad_gated * conv_q

    source_lanes = lax.all_to_all(
        source.reshape(1, length, devices, lane_width), "seq", split_axis=2, concat_axis=2, tiled=True
    )
    fetched, partner, source_lanes = lax.optimization_barrier((fetched, partner, source_lanes))
    grad_lanes = lax.all_to_all(
        grad_state.reshape(1, length, devices, lane_width), "seq", split_axis=2, concat_axis=2, tiled=True
    )
    filter_spectra = forward_spectra(filter_lanes, total)
    source_spectra = forward_spectra(source_lanes, total)
    kernel_real = filter_spectra[0, 0]
    kernel_imag = filter_spectra[1, 0]
    data_real = source_spectra[0, 0]
    data_imag = source_spectra[1, 0]
    long_spectra = jnp.stack(
        [data_real * kernel_real - data_imag * kernel_imag, data_real * kernel_imag + data_imag * kernel_real]
    )[:, None]
    long_back = inverse_signals(long_spectra, devices, total)
    grad_lanes, long_back = lax.optimization_barrier((grad_lanes, long_back))
    long_part = lax.all_to_all(long_back, "seq", split_axis=2, concat_axis=2, tiled=True)
    grad_spectra = forward_spectra(grad_lanes, total)
    grad_real = grad_spectra[0, 0]
    grad_imag = grad_spectra[1, 0]
    adjoint = jnp.stack(
        [grad_real * kernel_real + grad_imag * kernel_imag, grad_imag * kernel_real - grad_real * kernel_imag]
    )[:, None]
    grad_back = inverse_signals(adjoint, devices, total)

    mixer_state = long_part.reshape(length, channels) + skip_gain * source
    gated = (conv_q * mixer_state).astype(jnp.bfloat16)
    gated, grad_back = lax.optimization_barrier((gated, grad_back))
    grad_long = lax.all_to_all(grad_back, "seq", split_axis=2, concat_axis=2, tiled=True)
    mine = jnp.dot(gated, lax.dynamic_slice_in_dim(own_block, core * half_width, half_width, axis=1),
                   preferred_element_type=jnp.float32)
    other = jnp.dot(gated, lax.dynamic_slice_in_dim(own_block, (1 - core) * half_width, half_width, axis=1),
                    preferred_element_type=jnp.float32)
    for shift in range(1, groups):
        received = exchanged(gated, shift)
        mine = mine + jnp.dot(received, fetched[shift - 1], preferred_element_type=jnp.float32)
        other = other + jnp.dot(received, partner[shift - 1], preferred_element_type=jnp.float32)
    terms = jnp.where(core == 0, jnp.concatenate([mine, other], axis=1), jnp.concatenate([other, mine], axis=1))
    mixed = terms.astype(jnp.bfloat16)

    grad_q = grad_gated * mixer_state
    grad_source = grad_long.reshape(length, channels) + skip_gain * grad_state
    gradients = jnp.stack([grad_q, grad_source * conv_v, grad_source * conv_k])
    following = passed_along(gradients[:, :2, :], "seq", -1)
    grad_ext = jnp.concatenate([gradients, following], axis=1)
    stream_grads = (
        short_taps[:, 0, None, :] * grad_ext[:, :-2]
        + short_taps[:, 1, None, :] * grad_ext[:, 1:-1]
        + short_taps[:, 2, None, :] * grad_ext[:, 2:]
    )
    return (mixed, stream_grads.astype(jnp.bfloat16))


def solution(mesh):
    return jax.shard_map(
        on_device,
        mesh=mesh,
        in_specs=(
            P(None, "seq", "tp"),
            P(None, None, "tp"),
            P("seq", "tp"),
            P("tp"),
            P("tp", None),
            P("seq", None),
        ),
        out_specs=(P("seq", "tp"), P(None, "seq", "tp")),
        check_vma=False,
    )
```

```python
import math

import jax
import jax.numpy as jnp
from jax import lax
from jax.sharding import PartitionSpec as P

full_turn = 2.0 * math.pi
fast = lax.Precision.HIGH


def passed_along(x, axis, by):
    devices = lax.axis_size(axis)
    pairs = [(i, i + by) for i in range(devices) if 0 <= i + by < devices]
    return lax.ppermute(x, axis, pairs)


def angle_table(rows, cols, period):
    row_ids = jnp.arange(rows, dtype=jnp.int32)[:, None]
    col_ids = jnp.arange(cols, dtype=jnp.int32)[None, :]
    angles = (row_ids * col_ids % period).astype(jnp.float32) * (full_turn / period)
    return (jnp.cos(angles), jnp.sin(angles))


def forward_spectra(lanes, total):
    count = lanes.shape[2]
    length = lanes.shape[1]
    half = count + 1
    cosine, sine = angle_table(half, count, 2 * count)
    first = jnp.einsum("rkm,simc->rsikc", jnp.stack([cosine, -sine]), lanes, precision=fast)
    twist_cos, twist_sin = angle_table(length, half, total)
    twist_cos = twist_cos[:, :, None]
    twist_sin = twist_sin[:, :, None]
    real_part = first[0] * twist_cos + first[1] * twist_sin
    imag_part = first[1] * twist_cos - first[0] * twist_sin
    cos_b, sin_b = angle_table(length, length, length)
    table = jnp.stack([jnp.stack([cos_b, sin_b]), jnp.stack([-sin_b, cos_b])])
    return jnp.einsum(
        "rqji,qsikc->rsjkc", table, jnp.stack([real_part, imag_part]), precision=fast
    )


def inverse_signals(spectral, count, total):
    length = spectral.shape[2]
    half = spectral.shape[3]
    cos_b, sin_b = angle_table(length, length, length)
    table = jnp.stack([jnp.stack([cos_b, -sin_b]), jnp.stack([sin_b, cos_b])])
    block = jnp.einsum("rqij,qsjkc->rsikc", table, spectral, precision=fast)
    twist_cos, twist_sin = angle_table(length, half, total)
    twist_cos = twist_cos[:, :, None]
    twist_sin = twist_sin[:, :, None]
    real_part = block[0] * twist_cos - block[1] * twist_sin
    imag_part = block[0] * twist_sin + block[1] * twist_cos
    cosine, sine = angle_table(count, half, 2 * count)
    k_ids = jnp.arange(half, dtype=jnp.int32)[None, :]
    weight = jnp.where((k_ids == 0) | (k_ids == count), 1.0, 2.0) * (1.0 / total)
    last = jnp.stack([cosine * weight, -sine * weight])
    return jnp.einsum(
        "rmk,rsikc->simc", last, jnp.stack([real_part, imag_part]), precision=fast
    )


def on_device(streams, short_taps, filter_taps, skip_gain, w_out, cotangent):
    length = streams.shape[1]
    channels = streams.shape[2]
    devices = lax.axis_size("seq")
    groups = lax.axis_size("tp")
    total = 2 * length * devices
    lane_width = channels // devices
    features = w_out.shape[1] // groups
    me = lax.axis_index("tp")

    def exchanged(x, shift):
        return lax.ppermute(x, "tp", [(i, (i + shift) % groups) for i in range(groups)])

    core = lax.axis_index("seq") % 2
    half_width = features // 2
    own_block = lax.dynamic_slice_in_dim(w_out, me * features, features, axis=1)
    fetched = []
    for shift in range(1, groups):
        target = (me + shift) % groups
        piece = lax.dynamic_slice_in_dim(w_out, target * features + core * half_width, half_width, axis=1)
        fetched.append(exchanged(piece, shift))
    fetched = jnp.stack(fetched)
    partner = lax.ppermute(fetched, "seq", [(i, i ^ 1) for i in range(devices)])

    previous = passed_along(streams[:, -2:, :], "seq", 1)
    extended = jnp.concatenate([previous, streams], axis=1).astype(jnp.float32)
    convolved = (
        short_taps[:, 0, None, :] * extended[:, 2:]
        + short_taps[:, 1, None, :] * extended[:, 1:-1]
        + short_taps[:, 2, None, :] * extended[:, :-2]
    )
    conv_q = convolved[0]
    conv_k = convolved[1]
    conv_v = convolved[2]
    source = conv_k * conv_v
    grad_gated = lax.dot_general(
        cotangent, w_out, (((1,), (1,)), ((), ())), preferred_element_type=jnp.float32
    )
    grad_state = grad_gated * conv_q

    signals = jnp.stack([filter_taps, source, grad_state]).reshape(3, length, devices, lane_width)
    lanes = lax.all_to_all(signals, "seq", split_axis=2, concat_axis=2, tiled=True)
    fetched, partner, lanes = lax.optimization_barrier((fetched, partner, lanes))
    spectra = forward_spectra(lanes, total)
    kernel_real = spectra[0, 0]
    kernel_imag = spectra[1, 0]
    data_real = spectra[0, 1]
    data_imag = spectra[1, 1]
    grad_real = spectra[0, 2]
    grad_imag = spectra[1, 2]
    long_spectra = jnp.stack(
        [data_real * kernel_real - data_imag * kernel_imag, data_real * kernel_imag + data_imag * kernel_real]
    )[:, None]
    long_back = inverse_signals(long_spectra, devices, total)
    long_part = lax.all_to_all(long_back, "seq", split_axis=2, concat_axis=2, tiled=True)
    adjoint = jnp.stack(
        [grad_real * kernel_real + grad_imag * kernel_imag, grad_imag * kernel_real - grad_real * kernel_imag]
    )[:, None]
    grad_back = inverse_signals(adjoint, devices, total)

    mixer_state = long_part.reshape(length, channels) + skip_gain * source
    gated = (conv_q * mixer_state).astype(jnp.bfloat16)
    gated, grad_back = lax.optimization_barrier((gated, grad_back))
    grad_long = lax.all_to_all(grad_back, "seq", split_axis=2, concat_axis=2, tiled=True)
    mine = jnp.dot(gated, lax.dynamic_slice_in_dim(own_block, core * half_width, half_width, axis=1),
                   preferred_element_type=jnp.float32)
    other = jnp.dot(gated, lax.dynamic_slice_in_dim(own_block, (1 - core) * half_width, half_width, axis=1),
                    preferred_element_type=jnp.float32)
    for shift in range(1, groups):
        received = exchanged(gated, shift)
        mine = mine + jnp.dot(received, fetched[shift - 1], preferred_element_type=jnp.float32)
        other = other + jnp.dot(received, partner[shift - 1], preferred_element_type=jnp.float32)
    terms = jnp.where(core == 0, jnp.concatenate([mine, other], axis=1), jnp.concatenate([other, mine], axis=1))
    mixed = terms.astype(jnp.bfloat16)

    grad_q = grad_gated * mixer_state
    grad_source = grad_long.reshape(length, channels) + skip_gain * grad_state
    gradients = jnp.stack([grad_q, grad_source * conv_v, grad_source * conv_k])
    following = passed_along(gradients[:, :2, :], "seq", -1)
    grad_ext = jnp.concatenate([gradients, following], axis=1)
    stream_grads = (
        short_taps[:, 0, None, :] * grad_ext[:, :-2]
        + short_taps[:, 1, None, :] * grad_ext[:, 1:-1]
        + short_taps[:, 2, None, :] * grad_ext[:, 2:]
    )
    return (mixed, stream_grads.astype(jnp.bfloat16))


def solution(mesh):
    return jax.shard_map(
        on_device,
        mesh=mesh,
        in_specs=(
            P(None, "seq", "tp"),
            P(None, None, "tp"),
            P("seq", "tp"),
            P("tp"),
            P("tp", None),
            P("seq", None),
        ),
        out_specs=(P("seq", "tp"), P(None, "seq", "tp")),
        check_vma=False,
    )
```

```python
import math

import jax
import jax.numpy as jnp
from jax import lax
from jax.sharding import PartitionSpec as P

full_turn = 2.0 * math.pi
fast = lax.Precision.HIGH


def passed_along(x, axis, by):
    devices = lax.axis_size(axis)
    pairs = [(i, i + by) for i in range(devices) if 0 <= i + by < devices]
    return lax.ppermute(x, axis, pairs)


def angle_table(rows, cols, period):
    row_ids = jnp.arange(rows, dtype=jnp.int32)[:, None]
    col_ids = jnp.arange(cols, dtype=jnp.int32)[None, :]
    angles = (row_ids * col_ids % period).astype(jnp.float32) * (full_turn / period)
    return (jnp.cos(angles), jnp.sin(angles))


def forward_spectra(lanes, total):
    count = lanes.shape[2]
    length = lanes.shape[1]
    half = count + 1
    cosine, sine = angle_table(half, count, 2 * count)
    first = jnp.einsum("rkm,simc->rsikc", jnp.stack([cosine, -sine]), lanes, precision=fast)
    twist_cos, twist_sin = angle_table(length, half, total)
    twist_cos = twist_cos[:, :, None]
    twist_sin = twist_sin[:, :, None]
    real_part = first[0] * twist_cos + first[1] * twist_sin
    imag_part = first[1] * twist_cos - first[0] * twist_sin
    cos_b, sin_b = angle_table(length, length, length)
    table = jnp.stack([jnp.stack([cos_b, sin_b]), jnp.stack([-sin_b, cos_b])])
    return jnp.einsum(
        "rqji,qsikc->rsjkc", table, jnp.stack([real_part, imag_part]), precision=fast
    )


def inverse_signals(spectral, count, total):
    length = spectral.shape[2]
    half = spectral.shape[3]
    cos_b, sin_b = angle_table(length, length, length)
    table = jnp.stack([jnp.stack([cos_b, -sin_b]), jnp.stack([sin_b, cos_b])])
    block = jnp.einsum("rqij,qsjkc->rsikc", table, spectral, precision=fast)
    twist_cos, twist_sin = angle_table(length, half, total)
    twist_cos = twist_cos[:, :, None]
    twist_sin = twist_sin[:, :, None]
    real_part = block[0] * twist_cos - block[1] * twist_sin
    imag_part = block[0] * twist_sin + block[1] * twist_cos
    cosine, sine = angle_table(count, half, 2 * count)
    k_ids = jnp.arange(half, dtype=jnp.int32)[None, :]
    weight = jnp.where((k_ids == 0) | (k_ids == count), 1.0, 2.0) * (1.0 / total)
    last = jnp.stack([cosine * weight, -sine * weight])
    return jnp.einsum(
        "rmk,rsikc->simc", last, jnp.stack([real_part, imag_part]), precision=fast
    )


def on_device(streams, short_taps, filter_taps, skip_gain, w_out, cotangent):
    length = streams.shape[1]
    channels = streams.shape[2]
    devices = lax.axis_size("seq")
    groups = lax.axis_size("tp")
    total = 2 * length * devices
    lane_width = channels // devices
    features = w_out.shape[1] // groups
    me = lax.axis_index("tp")

    def exchanged(x, shift):
        return lax.ppermute(x, "tp", [(i, (i + shift) % groups) for i in range(groups)])

    core = lax.axis_index("seq") % 2
    half_width = features // 2
    own_block = lax.dynamic_slice_in_dim(w_out, me * features, features, axis=1)
    pieces = [
        lax.dynamic_slice_in_dim(w_out, ((me + shift) % groups) * features + core * half_width, half_width, axis=1)
        for shift in range(1, groups)
    ]

    previous = passed_along(streams[:, -2:, :], "seq", 1)
    extended = jnp.concatenate([previous, streams], axis=1).astype(jnp.float32)
    convolved = (
        short_taps[:, 0, None, :] * extended[:, 2:]
        + short_taps[:, 1, None, :] * extended[:, 1:-1]
        + short_taps[:, 2, None, :] * extended[:, :-2]
    )
    conv_q = convolved[0]
    conv_k = convolved[1]
    conv_v = convolved[2]
    source = conv_k * conv_v
    grad_gated = lax.dot_general(
        cotangent, w_out, (((1,), (1,)), ((), ())), preferred_element_type=jnp.float32
    )
    grad_state = grad_gated * conv_q

    signals = jnp.stack([filter_taps, source, grad_state]).reshape(3, length, devices, lane_width)
    lanes = lax.all_to_all(signals, "seq", split_axis=2, concat_axis=2, tiled=True)
    pieces, lanes = lax.optimization_barrier((pieces, lanes))
    fetched = jnp.stack([exchanged(piece, shift) for shift, piece in enumerate(pieces, 1)])
    partner = lax.ppermute(fetched, "seq", [(i, i ^ 1) for i in range(devices)])
    spectra = forward_spectra(lanes, total)
    kernel_real = spectra[0, 0]
    kernel_imag = spectra[1, 0]
    data_real = spectra[0, 1]
    data_imag = spectra[1, 1]
    grad_real = spectra[0, 2]
    grad_imag = spectra[1, 2]
    long_spectra = jnp.stack(
        [data_real * kernel_real - data_imag * kernel_imag, data_real * kernel_imag + data_imag * kernel_real]
    )[:, None]
    long_back = inverse_signals(long_spectra, devices, total)
    fetched, partner, long_back = lax.optimization_barrier((fetched, partner, long_back))
    long_part = lax.all_to_all(long_back, "seq", split_axis=2, concat_axis=2, tiled=True)
    adjoint = jnp.stack(
        [grad_real * kernel_real + grad_imag * kernel_imag, grad_imag * kernel_real - grad_real * kernel_imag]
    )[:, None]
    grad_back = inverse_signals(adjoint, devices, total)

    mixer_state = long_part.reshape(length, channels) + skip_gain * source
    gated = (conv_q * mixer_state).astype(jnp.bfloat16)
    gated, grad_back = lax.optimization_barrier((gated, grad_back))
    grad_long = lax.all_to_all(grad_back, "seq", split_axis=2, concat_axis=2, tiled=True)
    mine = jnp.dot(gated, lax.dynamic_slice_in_dim(own_block, core * half_width, half_width, axis=1),
                   preferred_element_type=jnp.float32)
    other = jnp.dot(gated, lax.dynamic_slice_in_dim(own_block, (1 - core) * half_width, half_width, axis=1),
                    preferred_element_type=jnp.float32)
    for shift in range(1, groups):
        received = exchanged(gated, shift)
        mine = mine + jnp.dot(received, fetched[shift - 1], preferred_element_type=jnp.float32)
        other = other + jnp.dot(received, partner[shift - 1], preferred_element_type=jnp.float32)
    terms = jnp.where(core == 0, jnp.concatenate([mine, other], axis=1), jnp.concatenate([other, mine], axis=1))
    mixed = terms.astype(jnp.bfloat16)

    grad_q = grad_gated * mixer_state
    grad_source = grad_long.reshape(length, channels) + skip_gain * grad_state
    gradients = jnp.stack([grad_q, grad_source * conv_v, grad_source * conv_k])
    following = passed_along(gradients[:, :2, :], "seq", -1)
    grad_ext = jnp.concatenate([gradients, following], axis=1)
    stream_grads = (
        short_taps[:, 0, None, :] * grad_ext[:, :-2]
        + short_taps[:, 1, None, :] * grad_ext[:, 1:-1]
        + short_taps[:, 2, None, :] * grad_ext[:, 2:]
    )
    return (mixed, stream_grads.astype(jnp.bfloat16))


def solution(mesh):
    return jax.shard_map(
        on_device,
        mesh=mesh,
        in_specs=(
            P(None, "seq", "tp"),
            P(None, None, "tp"),
            P("seq", "tp"),
            P("tp"),
            P("tp", None),
            P("seq", None),
        ),
        out_specs=(P("seq", "tp"), P(None, "seq", "tp")),
        check_vma=False,
    )
```

```python
import math

import jax
import jax.numpy as jnp
from jax import lax
from jax.sharding import PartitionSpec as P

full_turn = 2.0 * math.pi
fast = lax.Precision.HIGH


def passed_along(x, axis, by):
    devices = lax.axis_size(axis)
    pairs = [(i, i + by) for i in range(devices) if 0 <= i + by < devices]
    return lax.ppermute(x, axis, pairs)


def angle_table(rows, cols, period):
    row_ids = jnp.arange(rows, dtype=jnp.int32)[:, None]
    col_ids = jnp.arange(cols, dtype=jnp.int32)[None, :]
    angles = (row_ids * col_ids % period).astype(jnp.float32) * (full_turn / period)
    return (jnp.cos(angles), jnp.sin(angles))


def forward_spectra(lanes, total):
    count = lanes.shape[2]
    length = lanes.shape[1]
    half = count + 1
    cosine, sine = angle_table(half, count, 2 * count)
    first = jnp.einsum("rkm,simc->rsikc", jnp.stack([cosine, -sine]), lanes, precision=fast)
    twist_cos, twist_sin = angle_table(length, half, total)
    twist_cos = twist_cos[:, :, None]
    twist_sin = twist_sin[:, :, None]
    real_part = first[0] * twist_cos + first[1] * twist_sin
    imag_part = first[1] * twist_cos - first[0] * twist_sin
    cos_b, sin_b = angle_table(length, length, length)
    table = jnp.stack([jnp.stack([cos_b, sin_b]), jnp.stack([-sin_b, cos_b])])
    return jnp.einsum(
        "rqji,qsikc->rsjkc", table, jnp.stack([real_part, imag_part]), precision=fast
    )


def inverse_signals(spectral, count, total):
    length = spectral.shape[2]
    half = spectral.shape[3]
    cos_b, sin_b = angle_table(length, length, length)
    table = jnp.stack([jnp.stack([cos_b, -sin_b]), jnp.stack([sin_b, cos_b])])
    block = jnp.einsum("rqij,qsjkc->rsikc", table, spectral, precision=fast)
    twist_cos, twist_sin = angle_table(length, half, total)
    twist_cos = twist_cos[:, :, None]
    twist_sin = twist_sin[:, :, None]
    real_part = block[0] * twist_cos - block[1] * twist_sin
    imag_part = block[0] * twist_sin + block[1] * twist_cos
    cosine, sine = angle_table(count, half, 2 * count)
    k_ids = jnp.arange(half, dtype=jnp.int32)[None, :]
    weight = jnp.where((k_ids == 0) | (k_ids == count), 1.0, 2.0) * (1.0 / total)
    last = jnp.stack([cosine * weight, -sine * weight])
    return jnp.einsum(
        "rmk,rsikc->simc", last, jnp.stack([real_part, imag_part]), precision=fast
    )


def on_device(streams, short_taps, filter_taps, skip_gain, w_out, cotangent):
    length = streams.shape[1]
    channels = streams.shape[2]
    devices = lax.axis_size("seq")
    groups = lax.axis_size("tp")
    total = 2 * length * devices
    lane_width = channels // devices
    features = w_out.shape[1] // groups
    me = lax.axis_index("tp")

    def exchanged(x, shift):
        return lax.ppermute(x, "tp", [(i, (i + shift) % groups) for i in range(groups)])

    core = lax.axis_index("seq") % 2
    half_width = features // 2
    own_block = lax.dynamic_slice_in_dim(w_out, me * features, features, axis=1)
    pieces = [
        lax.dynamic_slice_in_dim(w_out, ((me + shift) % groups) * features + core * half_width, half_width, axis=1)
        for shift in range(1, groups)
    ]

    previous = passed_along(streams[:, -2:, :], "seq", 1)
    extended = jnp.concatenate([previous, streams], axis=1).astype(jnp.float32)
    convolved = (
        short_taps[:, 0, None, :] * extended[:, 2:]
        + short_taps[:, 1, None, :] * extended[:, 1:-1]
        + short_taps[:, 2, None, :] * extended[:, :-2]
    )
    conv_q = convolved[0]
    conv_k = convolved[1]
    conv_v = convolved[2]
    source = conv_k * conv_v
    grad_gated = lax.dot_general(
        cotangent, w_out, (((1,), (1,)), ((), ())), preferred_element_type=jnp.float32
    )
    grad_state = grad_gated * conv_q

    signals = jnp.stack([filter_taps, source]).reshape(2, length, devices, lane_width)
    lanes = lax.all_to_all(signals, "seq", split_axis=2, concat_axis=2, tiled=True)
    pieces, lanes = lax.optimization_barrier((pieces, lanes))
    fetched = jnp.stack([exchanged(piece, shift) for shift, piece in enumerate(pieces, 1)])
    partner = lax.ppermute(fetched, "seq", [(i, i ^ 1) for i in range(devices)])
    grad_lanes = lax.all_to_all(
        grad_state.reshape(1, length, devices, lane_width), "seq", split_axis=2, concat_axis=2, tiled=True
    )
    spectra = forward_spectra(lanes, total)
    kernel_real = spectra[0, 0]
    kernel_imag = spectra[1, 0]
    data_real = spectra[0, 1]
    data_imag = spectra[1, 1]
    long_spectra = jnp.stack(
        [data_real * kernel_real - data_imag * kernel_imag, data_real * kernel_imag + data_imag * kernel_real]
    )[:, None]
    long_back = inverse_signals(long_spectra, devices, total)
    grad_lanes, long_back = lax.optimization_barrier((grad_lanes, long_back))
    fetched, partner, long_back = lax.optimization_barrier((fetched, partner, long_back))
    long_part = lax.all_to_all(long_back, "seq", split_axis=2, concat_axis=2, tiled=True)
    grad_spectra = forward_spectra(grad_lanes, total)
    grad_real = grad_spectra[0, 0]
    grad_imag = grad_spectra[1, 0]
    adjoint = jnp.stack(
        [grad_real * kernel_real + grad_imag * kernel_imag, grad_imag * kernel_real - grad_real * kernel_imag]
    )[:, None]
    grad_back = inverse_signals(adjoint, devices, total)

    mixer_state = long_part.reshape(length, channels) + skip_gain * source
    gated = (conv_q * mixer_state).astype(jnp.bfloat16)
    gated, grad_back = lax.optimization_barrier((gated, grad_back))
    grad_long = lax.all_to_all(grad_back, "seq", split_axis=2, concat_axis=2, tiled=True)
    mine = jnp.dot(gated, lax.dynamic_slice_in_dim(own_block, core * half_width, half_width, axis=1),
                   preferred_element_type=jnp.float32)
    other = jnp.dot(gated, lax.dynamic_slice_in_dim(own_block, (1 - core) * half_width, half_width, axis=1),
                    preferred_element_type=jnp.float32)
    for shift in range(1, groups):
        received = exchanged(gated, shift)
        mine = mine + jnp.dot(received, fetched[shift - 1], preferred_element_type=jnp.float32)
        other = other + jnp.dot(received, partner[shift - 1], preferred_element_type=jnp.float32)
    terms = jnp.where(core == 0, jnp.concatenate([mine, other], axis=1), jnp.concatenate([other, mine], axis=1))
    mixed = terms.astype(jnp.bfloat16)

    grad_q = grad_gated * mixer_state
    grad_source = grad_long.reshape(length, channels) + skip_gain * grad_state
    gradients = jnp.stack([grad_q, grad_source * conv_v, grad_source * conv_k])
    following = passed_along(gradients[:, :2, :], "seq", -1)
    grad_ext = jnp.concatenate([gradients, following], axis=1)
    stream_grads = (
        short_taps[:, 0, None, :] * grad_ext[:, :-2]
        + short_taps[:, 1, None, :] * grad_ext[:, 1:-1]
        + short_taps[:, 2, None, :] * grad_ext[:, 2:]
    )
    return (mixed, stream_grads.astype(jnp.bfloat16))


def solution(mesh):
    return jax.shard_map(
        on_device,
        mesh=mesh,
        in_specs=(
            P(None, "seq", "tp"),
            P(None, None, "tp"),
            P("seq", "tp"),
            P("tp"),
            P("tp", None),
            P("seq", None),
        ),
        out_specs=(P("seq", "tp"), P(None, "seq", "tp")),
        check_vma=False,
    )
```

```python
import math

import jax
import jax.numpy as jnp
from jax import lax
from jax.sharding import PartitionSpec as P

full_turn = 2.0 * math.pi
fast = lax.Precision.HIGH


def passed_along(x, axis, by):
    devices = lax.axis_size(axis)
    pairs = [(i, i + by) for i in range(devices) if 0 <= i + by < devices]
    return lax.ppermute(x, axis, pairs)


def angle_table(rows, cols, period):
    row_ids = jnp.arange(rows, dtype=jnp.int32)[:, None]
    col_ids = jnp.arange(cols, dtype=jnp.int32)[None, :]
    angles = (row_ids * col_ids % period).astype(jnp.float32) * (full_turn / period)
    return (jnp.cos(angles), jnp.sin(angles))


def forward_spectra(lanes, total):
    count = lanes.shape[2]
    length = lanes.shape[1]
    half = count + 1
    cosine, sine = angle_table(half, count, 2 * count)
    first = jnp.einsum("rkm,simc->rsikc", jnp.stack([cosine, -sine]), lanes, precision=fast)
    twist_cos, twist_sin = angle_table(length, half, total)
    twist_cos = twist_cos[:, :, None]
    twist_sin = twist_sin[:, :, None]
    real_part = first[0] * twist_cos + first[1] * twist_sin
    imag_part = first[1] * twist_cos - first[0] * twist_sin
    cos_b, sin_b = angle_table(length, length, length)
    table = jnp.stack([cos_b - sin_b, cos_b, -sin_b])
    parts = jnp.stack([real_part, imag_part - real_part, real_part + imag_part])
    products = jnp.einsum("pji,psikc->psjkc", table, parts, precision=fast)
    return jnp.stack([products[0] - products[2], products[0] + products[1]])


def inverse_signals(spectral, count, total):
    length = spectral.shape[2]
    half = spectral.shape[3]
    cos_b, sin_b = angle_table(length, length, length)
    table = jnp.stack([cos_b + sin_b, cos_b, sin_b])
    parts = jnp.stack([spectral[0], spectral[1] - spectral[0], spectral[0] + spectral[1]])
    products = jnp.einsum("pij,psjkc->psikc", table, parts, precision=fast)
    block = jnp.stack([products[0] - products[2], products[0] + products[1]])
    twist_cos, twist_sin = angle_table(length, half, total)
    twist_cos = twist_cos[:, :, None]
    twist_sin = twist_sin[:, :, None]
    real_part = block[0] * twist_cos - block[1] * twist_sin
    imag_part = block[0] * twist_sin + block[1] * twist_cos
    cosine, sine = angle_table(count, half, 2 * count)
    k_ids = jnp.arange(half, dtype=jnp.int32)[None, :]
    weight = jnp.where((k_ids == 0) | (k_ids == count), 1.0, 2.0) * (1.0 / total)
    last = jnp.stack([cosine * weight, -sine * weight])
    return jnp.einsum(
        "rmk,rsikc->simc", last, jnp.stack([real_part, imag_part]), precision=fast
    )


def on_device(streams, short_taps, filter_taps, skip_gain, w_out, cotangent):
    length = streams.shape[1]
    channels = streams.shape[2]
    devices = lax.axis_size("seq")
    groups = lax.axis_size("tp")
    total = 2 * length * devices
    lane_width = channels // devices
    features = w_out.shape[1] // groups
    me = lax.axis_index("tp")

    def exchanged(x, shift):
        return lax.ppermute(x, "tp", [(i, (i + shift) % groups) for i in range(groups)])

    core = lax.axis_index("seq") % 2
    half_width = features // 2
    own_block = lax.dynamic_slice_in_dim(w_out, me * features, features, axis=1)
    pieces = [
        lax.dynamic_slice_in_dim(w_out, ((me + shift) % groups) * features + core * half_width, half_width, axis=1)
        for shift in range(1, groups)
    ]

    previous = passed_along(streams[:, -2:, :], "seq", 1)
    extended = jnp.concatenate([previous, streams], axis=1).astype(jnp.float32)
    convolved = (
        short_taps[:, 0, None, :] * extended[:, 2:]
        + short_taps[:, 1, None, :] * extended[:, 1:-1]
        + short_taps[:, 2, None, :] * extended[:, :-2]
    )
    conv_q = convolved[0]
    conv_k = convolved[1]
    conv_v = convolved[2]
    source = conv_k * conv_v
    grad_gated = lax.dot_general(
        cotangent, w_out, (((1,), (1,)), ((), ())), preferred_element_type=jnp.float32
    )
    grad_state = grad_gated * conv_q

    signals = jnp.stack([filter_taps, source, grad_state]).reshape(3, length, devices, lane_width)
    lanes = lax.all_to_all(signals, "seq", split_axis=2, concat_axis=2, tiled=True)
    pieces, lanes = lax.optimization_barrier((pieces, lanes))
    fetched = jnp.stack([exchanged(piece, shift) for shift, piece in enumerate(pieces, 1)])
    partner = lax.ppermute(fetched, "seq", [(i, i ^ 1) for i in range(devices)])
    spectra = forward_spectra(lanes, total)
    kernel_real = spectra[0, 0]
    kernel_imag = spectra[1, 0]
    data_real = spectra[0, 1]
    data_imag = spectra[1, 1]
    grad_real = spectra[0, 2]
    grad_imag = spectra[1, 2]
    long_spectra = jnp.stack(
        [data_real * kernel_real - data_imag * kernel_imag, data_real * kernel_imag + data_imag * kernel_real]
    )[:, None]
    long_back = inverse_signals(long_spectra, devices, total)
    fetched, partner, long_back = lax.optimization_barrier((fetched, partner, long_back))
    long_part = lax.all_to_all(long_back, "seq", split_axis=2, concat_axis=2, tiled=True)
    adjoint = jnp.stack(
        [grad_real * kernel_real + grad_imag * kernel_imag, grad_imag * kernel_real - grad_real * kernel_imag]
    )[:, None]
    grad_back = inverse_signals(adjoint, devices, total)

    mixer_state = long_part.reshape(length, channels) + skip_gain * source
    gated = (conv_q * mixer_state).astype(jnp.bfloat16)
    gated, grad_back = lax.optimization_barrier((gated, grad_back))
    grad_long = lax.all_to_all(grad_back, "seq", split_axis=2, concat_axis=2, tiled=True)
    mine = jnp.dot(gated, lax.dynamic_slice_in_dim(own_block, core * half_width, half_width, axis=1),
                   preferred_element_type=jnp.float32)
    other = jnp.dot(gated, lax.dynamic_slice_in_dim(own_block, (1 - core) * half_width, half_width, axis=1),
                    preferred_element_type=jnp.float32)
    for shift in range(1, groups):
        received = exchanged(gated, shift)
        mine = mine + jnp.dot(received, fetched[shift - 1], preferred_element_type=jnp.float32)
        other = other + jnp.dot(received, partner[shift - 1], preferred_element_type=jnp.float32)
    terms = jnp.where(core == 0, jnp.concatenate([mine, other], axis=1), jnp.concatenate([other, mine], axis=1))
    mixed = terms.astype(jnp.bfloat16)

    grad_q = grad_gated * mixer_state
    grad_source = grad_long.reshape(length, channels) + skip_gain * grad_state
    gradients = jnp.stack([grad_q, grad_source * conv_v, grad_source * conv_k])
    following = passed_along(gradients[:, :2, :], "seq", -1)
    grad_ext = jnp.concatenate([gradients, following], axis=1)
    stream_grads = (
        short_taps[:, 0, None, :] * grad_ext[:, :-2]
        + short_taps[:, 1, None, :] * grad_ext[:, 1:-1]
        + short_taps[:, 2, None, :] * grad_ext[:, 2:]
    )
    return (mixed, stream_grads.astype(jnp.bfloat16))


def solution(mesh):
    return jax.shard_map(
        on_device,
        mesh=mesh,
        in_specs=(
            P(None, "seq", "tp"),
            P(None, None, "tp"),
            P("seq", "tp"),
            P("tp"),
            P("tp", None),
            P("seq", None),
        ),
        out_specs=(P("seq", "tp"), P(None, "seq", "tp")),
        check_vma=False,
    )
```

```python
import math

import jax
import jax.numpy as jnp
from jax import lax
from jax.sharding import PartitionSpec as P

full_turn = 2.0 * math.pi
fast = lax.Precision.HIGH


def passed_along(x, axis, by):
    devices = lax.axis_size(axis)
    pairs = [(i, i + by) for i in range(devices) if 0 <= i + by < devices]
    return lax.ppermute(x, axis, pairs)


def angle_table(rows, cols, period):
    row_ids = jnp.arange(rows, dtype=jnp.int32)[:, None]
    col_ids = jnp.arange(cols, dtype=jnp.int32)[None, :]
    angles = (row_ids * col_ids % period).astype(jnp.float32) * (full_turn / period)
    return (jnp.cos(angles), jnp.sin(angles))


def forward_spectra(lanes, total):
    count = lanes.shape[2]
    length = lanes.shape[1]
    half = count + 1
    cosine, sine = angle_table(half, count, 2 * count)
    first = jnp.einsum("rkm,simc->rsikc", jnp.stack([cosine, -sine]), lanes, precision=fast)
    twist_cos, twist_sin = angle_table(length, half, total)
    twist_cos = twist_cos[:, :, None]
    twist_sin = twist_sin[:, :, None]
    real_part = first[0] * twist_cos + first[1] * twist_sin
    imag_part = first[1] * twist_cos - first[0] * twist_sin
    cos_b, sin_b = angle_table(length, length, length)
    table = jnp.stack([cos_b - sin_b, cos_b, -sin_b])
    parts = jnp.stack([real_part, imag_part - real_part, real_part + imag_part])
    products = jnp.einsum("pji,psikc->psjkc", table, parts, precision=fast)
    return jnp.stack([products[0] - products[2], products[0] + products[1]])


def inverse_signals(spectral, count, total):
    length = spectral.shape[2]
    half = spectral.shape[3]
    cos_b, sin_b = angle_table(length, length, length)
    table = jnp.stack([cos_b + sin_b, cos_b, sin_b])
    parts = jnp.stack([spectral[0], spectral[1] - spectral[0], spectral[0] + spectral[1]])
    products = jnp.einsum("pij,psjkc->psikc", table, parts, precision=fast)
    block = jnp.stack([products[0] - products[2], products[0] + products[1]])
    twist_cos, twist_sin = angle_table(length, half, total)
    twist_cos = twist_cos[:, :, None]
    twist_sin = twist_sin[:, :, None]
    real_part = block[0] * twist_cos - block[1] * twist_sin
    imag_part = block[0] * twist_sin + block[1] * twist_cos
    cosine, sine = angle_table(count, half, 2 * count)
    k_ids = jnp.arange(half, dtype=jnp.int32)[None, :]
    weight = jnp.where((k_ids == 0) | (k_ids == count), 1.0, 2.0) * (1.0 / total)
    last = jnp.stack([cosine * weight, -sine * weight])
    return jnp.einsum(
        "rmk,rsikc->simc", last, jnp.stack([real_part, imag_part]), precision=fast
    )


def on_device(streams, short_taps, filter_taps, skip_gain, w_out, cotangent):
    length = streams.shape[1]
    channels = streams.shape[2]
    devices = lax.axis_size("seq")
    groups = lax.axis_size("tp")
    total = 2 * length * devices
    lane_width = channels // devices
    features = w_out.shape[1] // groups
    me = lax.axis_index("tp")

    def exchanged(x, shift):
        return lax.ppermute(x, "tp", [(i, (i + shift) % groups) for i in range(groups)])

    core = lax.axis_index("seq") % 2
    half_width = features // 2
    own_block = lax.dynamic_slice_in_dim(w_out, me * features, features, axis=1)
    pieces = [
        lax.dynamic_slice_in_dim(w_out, ((me + shift) % groups) * features + core * half_width, half_width, axis=1)
        for shift in range(1, groups)
    ]

    previous = passed_along(streams[:, -2:, :], "seq", 1)
    extended = jnp.concatenate([previous, streams], axis=1).astype(jnp.float32)
    convolved = (
        short_taps[:, 0, None, :] * extended[:, 2:]
        + short_taps[:, 1, None, :] * extended[:, 1:-1]
        + short_taps[:, 2, None, :] * extended[:, :-2]
    )
    conv_q = convolved[0]
    conv_k = convolved[1]
    conv_v = convolved[2]
    source = conv_k * conv_v
    grad_gated = lax.dot_general(
        cotangent, w_out, (((1,), (1,)), ((), ())), preferred_element_type=jnp.float32
    )
    grad_state = grad_gated * conv_q

    signals = jnp.stack([filter_taps, source, grad_state]).reshape(3, length, devices, lane_width)
    lanes = lax.all_to_all(signals, "seq", split_axis=2, concat_axis=2, tiled=True)
    fetched = jnp.stack([exchanged(piece, shift) for shift, piece in enumerate(pieces, 1)])
    partner = lax.ppermute(fetched, "seq", [(i, i ^ 1) for i in range(devices)])
    spectra = forward_spectra(lanes, total)
    kernel_real = spectra[0, 0]
    kernel_imag = spectra[1, 0]
    data_real = spectra[0, 1]
    data_imag = spectra[1, 1]
    grad_real = spectra[0, 2]
    grad_imag = spectra[1, 2]
    long_spectra = jnp.stack(
        [data_real * kernel_real - data_imag * kernel_imag, data_real * kernel_imag + data_imag * kernel_real]
    )[:, None]
    long_back = inverse_signals(long_spectra, devices, total)
    fetched, partner, long_back = lax.optimization_barrier((fetched, partner, long_back))
    long_part = lax.all_to_all(long_back, "seq", split_axis=2, concat_axis=2, tiled=True)
    adjoint = jnp.stack(
        [grad_real * kernel_real + grad_imag * kernel_imag, grad_imag * kernel_real - grad_real * kernel_imag]
    )[:, None]
    grad_back = inverse_signals(adjoint, devices, total)

    mixer_state = long_part.reshape(length, channels) + skip_gain * source
    gated = (conv_q * mixer_state).astype(jnp.bfloat16)
    gated, grad_back = lax.optimization_barrier((gated, grad_back))
    grad_long = lax.all_to_all(grad_back, "seq", split_axis=2, concat_axis=2, tiled=True)
    mine = jnp.dot(gated, lax.dynamic_slice_in_dim(own_block, core * half_width, half_width, axis=1),
                   preferred_element_type=jnp.float32)
    other = jnp.dot(gated, lax.dynamic_slice_in_dim(own_block, (1 - core) * half_width, half_width, axis=1),
                    preferred_element_type=jnp.float32)
    for shift in range(1, groups):
        received = exchanged(gated, shift)
        mine = mine + jnp.dot(received, fetched[shift - 1], preferred_element_type=jnp.float32)
        other = other + jnp.dot(received, partner[shift - 1], preferred_element_type=jnp.float32)
    terms = jnp.where(core == 0, jnp.concatenate([mine, other], axis=1), jnp.concatenate([other, mine], axis=1))
    mixed = terms.astype(jnp.bfloat16)

    grad_q = grad_gated * mixer_state
    grad_source = grad_long.reshape(length, channels) + skip_gain * grad_state
    gradients = jnp.stack([grad_q, grad_source * conv_v, grad_source * conv_k])
    following = passed_along(gradients[:, :2, :], "seq", -1)
    grad_ext = jnp.concatenate([gradients, following], axis=1)
    stream_grads = (
        short_taps[:, 0, None, :] * grad_ext[:, :-2]
        + short_taps[:, 1, None, :] * grad_ext[:, 1:-1]
        + short_taps[:, 2, None, :] * grad_ext[:, 2:]
    )
    return (mixed, stream_grads.astype(jnp.bfloat16))


def solution(mesh):
    return jax.shard_map(
        on_device,
        mesh=mesh,
        in_specs=(
            P(None, "seq", "tp"),
            P(None, None, "tp"),
            P("seq", "tp"),
            P("tp"),
            P("tp", None),
            P("seq", None),
        ),
        out_specs=(P("seq", "tp"), P(None, "seq", "tp")),
        check_vma=False,
    )
```

```python
import math

import jax
import jax.numpy as jnp
from jax import lax
from jax.sharding import PartitionSpec as P

full_turn = 2.0 * math.pi
fast = lax.Precision.HIGH


def passed_along(x, axis, by):
    devices = lax.axis_size(axis)
    pairs = [(i, i + by) for i in range(devices) if 0 <= i + by < devices]
    return lax.ppermute(x, axis, pairs)


def angle_table(rows, cols, period):
    row_ids = jnp.arange(rows, dtype=jnp.int32)[:, None]
    col_ids = jnp.arange(cols, dtype=jnp.int32)[None, :]
    angles = (row_ids * col_ids % period).astype(jnp.float32) * (full_turn / period)
    return (jnp.cos(angles), jnp.sin(angles))


def forward_spectra(lanes, total):
    count = lanes.shape[2]
    length = lanes.shape[1]
    half = count + 1
    cosine, sine = angle_table(half, count, 2 * count)
    first = jnp.einsum("rkm,simc->rsikc", jnp.stack([cosine, -sine]), lanes, precision=fast)
    twist_cos, twist_sin = angle_table(length, half, total)
    twist_cos = twist_cos[:, :, None]
    twist_sin = twist_sin[:, :, None]
    real_part = first[0] * twist_cos + first[1] * twist_sin
    imag_part = first[1] * twist_cos - first[0] * twist_sin
    cos_b, sin_b = angle_table(length, length, length)
    table = jnp.stack([cos_b - sin_b, cos_b, -sin_b])
    parts = jnp.stack([real_part, imag_part - real_part, real_part + imag_part])
    products = jnp.einsum("pji,psikc->psjkc", table, parts, precision=fast)
    return jnp.stack([products[0] - products[2], products[0] + products[1]])


def inverse_signals(spectral, count, total):
    length = spectral.shape[2]
    half = spectral.shape[3]
    cos_b, sin_b = angle_table(length, length, length)
    table = jnp.stack([cos_b + sin_b, cos_b, sin_b])
    parts = jnp.stack([spectral[0], spectral[1] - spectral[0], spectral[0] + spectral[1]])
    products = jnp.einsum("pij,psjkc->psikc", table, parts, precision=fast)
    block = jnp.stack([products[0] - products[2], products[0] + products[1]])
    twist_cos, twist_sin = angle_table(length, half, total)
    twist_cos = twist_cos[:, :, None]
    twist_sin = twist_sin[:, :, None]
    real_part = block[0] * twist_cos - block[1] * twist_sin
    imag_part = block[0] * twist_sin + block[1] * twist_cos
    cosine, sine = angle_table(count, half, 2 * count)
    k_ids = jnp.arange(half, dtype=jnp.int32)[None, :]
    weight = jnp.where((k_ids == 0) | (k_ids == count), 1.0, 2.0) * (1.0 / total)
    last = jnp.stack([cosine * weight, -sine * weight])
    return jnp.einsum(
        "rmk,rsikc->simc", last, jnp.stack([real_part, imag_part]), precision=fast
    )


def on_device(streams, short_taps, filter_taps, skip_gain, w_out, cotangent):
    length = streams.shape[1]
    channels = streams.shape[2]
    devices = lax.axis_size("seq")
    groups = lax.axis_size("tp")
    total = 2 * length * devices
    lane_width = channels // devices
    features = w_out.shape[1] // groups
    me = lax.axis_index("tp")

    def exchanged(x, shift):
        return lax.ppermute(x, "tp", [(i, (i + shift) % groups) for i in range(groups)])

    core = lax.axis_index("seq") % 2
    half_width = features // 2
    own_block = lax.dynamic_slice_in_dim(w_out, me * features, features, axis=1)
    pieces = [
        lax.dynamic_slice_in_dim(w_out, ((me + shift) % groups) * features + core * half_width, half_width, axis=1)
        for shift in range(1, groups)
    ]

    previous = passed_along(streams[:, -2:, :], "seq", 1)
    extended = jnp.concatenate([previous, streams], axis=1).astype(jnp.float32)
    convolved = (
        short_taps[:, 0, None, :] * extended[:, 2:]
        + short_taps[:, 1, None, :] * extended[:, 1:-1]
        + short_taps[:, 2, None, :] * extended[:, :-2]
    )
    conv_q = convolved[0]
    conv_k = convolved[1]
    conv_v = convolved[2]
    source = conv_k * conv_v
    grad_gated = lax.dot_general(
        cotangent, w_out, (((1,), (1,)), ((), ())), preferred_element_type=jnp.float32
    )
    grad_state = grad_gated * conv_q

    signals = jnp.stack([filter_taps, source, grad_state]).reshape(3, length, devices, lane_width)
    lanes = lax.all_to_all(signals, "seq", split_axis=2, concat_axis=2, tiled=True)
    fetched = jnp.stack([exchanged(piece, shift) for shift, piece in enumerate(pieces, 1)])
    partner = lax.ppermute(fetched, "seq", [(i, i ^ 1) for i in range(devices)])
    spectra = forward_spectra(lanes, total)
    kernel_real = spectra[0, 0]
    kernel_imag = spectra[1, 0]
    data_real = spectra[0, 1]
    data_imag = spectra[1, 1]
    grad_real = spectra[0, 2]
    grad_imag = spectra[1, 2]
    long_spectra = jnp.stack(
        [data_real * kernel_real - data_imag * kernel_imag, data_real * kernel_imag + data_imag * kernel_real]
    )[:, None]
    long_back = inverse_signals(long_spectra, devices, total)
    fetched, partner, long_back = lax.optimization_barrier((fetched, partner, long_back))
    long_part = lax.all_to_all(long_back, "seq", split_axis=2, concat_axis=2, tiled=True)
    adjoint = jnp.stack(
        [grad_real * kernel_real + grad_imag * kernel_imag, grad_imag * kernel_real - grad_real * kernel_imag]
    )[:, None]
    grad_back = inverse_signals(adjoint, devices, total)

    mixer_state = long_part.reshape(length, channels) + skip_gain * source
    gated = (conv_q * mixer_state).astype(jnp.bfloat16)
    gated, grad_back = lax.optimization_barrier((gated, grad_back))
    grad_long = lax.all_to_all(grad_back, "seq", split_axis=2, concat_axis=2, tiled=True)
    blocks = [own_block]
    for shift in range(1, groups):
        mine, other = fetched[shift - 1], partner[shift - 1]
        blocks.append(
            jnp.where(core == 0, jnp.concatenate([mine, other], axis=1), jnp.concatenate([other, mine], axis=1))
        )
    gathered = jnp.concatenate([gated] + [exchanged(gated, shift) for shift in range(1, groups)], axis=1)
    terms = jnp.dot(gathered, jnp.concatenate(blocks, axis=0), preferred_element_type=jnp.float32)
    mixed = terms.astype(jnp.bfloat16)

    grad_q = grad_gated * mixer_state
    grad_source = grad_long.reshape(length, channels) + skip_gain * grad_state
    gradients = jnp.stack([grad_q, grad_source * conv_v, grad_source * conv_k])
    following = passed_along(gradients[:, :2, :], "seq", -1)
    grad_ext = jnp.concatenate([gradients, following], axis=1)
    stream_grads = (
        short_taps[:, 0, None, :] * grad_ext[:, :-2]
        + short_taps[:, 1, None, :] * grad_ext[:, 1:-1]
        + short_taps[:, 2, None, :] * grad_ext[:, 2:]
    )
    return (mixed, stream_grads.astype(jnp.bfloat16))


def solution(mesh):
    return jax.shard_map(
        on_device,
        mesh=mesh,
        in_specs=(
            P(None, "seq", "tp"),
            P(None, None, "tp"),
            P("seq", "tp"),
            P("tp"),
            P("tp", None),
            P("seq", None),
        ),
        out_specs=(P("seq", "tp"), P(None, "seq", "tp")),
        check_vma=False,
    )
```

```python
import math

import jax
import jax.numpy as jnp
from jax import lax
from jax.sharding import PartitionSpec as P

full_turn = 2.0 * math.pi
fast = lax.Precision.HIGH


def passed_along(x, axis, by):
    devices = lax.axis_size(axis)
    pairs = [(i, i + by) for i in range(devices) if 0 <= i + by < devices]
    return lax.ppermute(x, axis, pairs)


def angle_table(rows, cols, period):
    row_ids = jnp.arange(rows, dtype=jnp.int32)[:, None]
    col_ids = jnp.arange(cols, dtype=jnp.int32)[None, :]
    angles = (row_ids * col_ids % period).astype(jnp.float32) * (full_turn / period)
    return (jnp.cos(angles), jnp.sin(angles))


def forward_spectra(lanes, total):
    count = lanes.shape[2]
    length = lanes.shape[1]
    half = count + 1
    cosine, sine = angle_table(half, count, 2 * count)
    first = jnp.einsum("rkm,simc->rsikc", jnp.stack([cosine, -sine]), lanes, precision=fast)
    twist_cos, twist_sin = angle_table(length, half, total)
    twist_cos = twist_cos[:, :, None]
    twist_sin = twist_sin[:, :, None]
    real_part = first[0] * twist_cos + first[1] * twist_sin
    imag_part = first[1] * twist_cos - first[0] * twist_sin
    cos_b, sin_b = angle_table(length, length, length)
    table = jnp.stack([cos_b - sin_b, cos_b, -sin_b])
    parts = jnp.stack([real_part, imag_part - real_part, real_part + imag_part])
    products = jnp.einsum("pji,psikc->psjkc", table, parts, precision=fast)
    return jnp.stack([products[0] - products[2], products[0] + products[1]])


def inverse_signals(spectral, count, total):
    length = spectral.shape[2]
    half = spectral.shape[3]
    cos_b, sin_b = angle_table(length, length, length)
    table = jnp.stack([cos_b + sin_b, cos_b, sin_b])
    parts = jnp.stack([spectral[0], spectral[1] - spectral[0], spectral[0] + spectral[1]])
    products = jnp.einsum("pij,psjkc->psikc", table, parts, precision=fast)
    block = jnp.stack([products[0] - products[2], products[0] + products[1]])
    twist_cos, twist_sin = angle_table(length, half, total)
    twist_cos = twist_cos[:, :, None]
    twist_sin = twist_sin[:, :, None]
    real_part = block[0] * twist_cos - block[1] * twist_sin
    imag_part = block[0] * twist_sin + block[1] * twist_cos
    cosine, sine = angle_table(count, half, 2 * count)
    k_ids = jnp.arange(half, dtype=jnp.int32)[None, :]
    weight = jnp.where((k_ids == 0) | (k_ids == count), 1.0, 2.0) * (1.0 / total)
    last = jnp.stack([cosine * weight, -sine * weight])
    return jnp.einsum(
        "rmk,rsikc->simc", last, jnp.stack([real_part, imag_part]), precision=fast
    )


def on_device(streams, short_taps, filter_taps, skip_gain, w_out, cotangent):
    length = streams.shape[1]
    channels = streams.shape[2]
    devices = lax.axis_size("seq")
    groups = lax.axis_size("tp")
    total = 2 * length * devices
    lane_width = channels // devices
    features = w_out.shape[1] // groups
    me = lax.axis_index("tp")

    def exchanged(x, shift):
        return lax.ppermute(x, "tp", [(i, (i + shift) % groups) for i in range(groups)])

    core = lax.axis_index("seq") % 2
    half_width = features // 2
    own_block = lax.dynamic_slice_in_dim(w_out, me * features, features, axis=1)
    pieces = [
        lax.dynamic_slice_in_dim(w_out, ((me + shift) % groups) * features + core * half_width, half_width, axis=1)
        for shift in range(1, groups)
    ]

    previous = passed_along(streams[:, -2:, :], "seq", 1)
    extended = jnp.concatenate([previous, streams], axis=1).astype(jnp.float32)
    convolved = (
        short_taps[:, 0, None, :] * extended[:, 2:]
        + short_taps[:, 1, None, :] * extended[:, 1:-1]
        + short_taps[:, 2, None, :] * extended[:, :-2]
    )
    conv_q = convolved[0]
    conv_k = convolved[1]
    conv_v = convolved[2]
    source = conv_k * conv_v
    grad_gated = lax.dot_general(
        cotangent, w_out, (((1,), (1,)), ((), ())), preferred_element_type=jnp.float32
    )
    grad_state = grad_gated * conv_q

    signals = jnp.stack([filter_taps, source, grad_state]).reshape(3, length, devices, lane_width)
    lanes = lax.all_to_all(signals, "seq", split_axis=2, concat_axis=2, tiled=True)
    fetched = jnp.stack([exchanged(piece, shift) for shift, piece in enumerate(pieces, 1)])
    partner = lax.ppermute(fetched, "seq", [(i, i ^ 1) for i in range(devices)])
    spectra = forward_spectra(lanes, total)
    kernel_real = spectra[0, 0]
    kernel_imag = spectra[1, 0]
    data_real = spectra[0, 1]
    data_imag = spectra[1, 1]
    grad_real = spectra[0, 2]
    grad_imag = spectra[1, 2]
    long_spectra = jnp.stack(
        [data_real * kernel_real - data_imag * kernel_imag, data_real * kernel_imag + data_imag * kernel_real]
    )[:, None]
    long_back = inverse_signals(long_spectra, devices, total)
    fetched, partner, long_back = lax.optimization_barrier((fetched, partner, long_back))
    long_part = lax.all_to_all(long_back, "seq", split_axis=2, concat_axis=2, tiled=True)
    adjoint = jnp.stack(
        [grad_real * kernel_real + grad_imag * kernel_imag, grad_imag * kernel_real - grad_real * kernel_imag]
    )[:, None]
    grad_back = inverse_signals(adjoint, devices, total)

    mixer_state = long_part.reshape(length, channels) + skip_gain * source
    gated = (conv_q * mixer_state).astype(jnp.bfloat16)
    blocks = [own_block]
    for shift in range(1, groups):
        mine, other = fetched[shift - 1], partner[shift - 1]
        blocks.append(
            jnp.where(core == 0, jnp.concatenate([mine, other], axis=1), jnp.concatenate([other, mine], axis=1))
        )
    stacked = jnp.concatenate(blocks, axis=0)
    gated, stacked, grad_back = lax.optimization_barrier((gated, stacked, grad_back))
    grad_long = lax.all_to_all(grad_back, "seq", split_axis=2, concat_axis=2, tiled=True)
    gathered = jnp.concatenate([gated] + [exchanged(gated, shift) for shift in range(1, groups)], axis=1)
    terms = jnp.dot(gathered, stacked, preferred_element_type=jnp.float32)
    mixed = terms.astype(jnp.bfloat16)

    grad_q = grad_gated * mixer_state
    grad_source = grad_long.reshape(length, channels) + skip_gain * grad_state
    gradients = jnp.stack([grad_q, grad_source * conv_v, grad_source * conv_k])
    following = passed_along(gradients[:, :2, :], "seq", -1)
    grad_ext = jnp.concatenate([gradients, following], axis=1)
    stream_grads = (
        short_taps[:, 0, None, :] * grad_ext[:, :-2]
        + short_taps[:, 1, None, :] * grad_ext[:, 1:-1]
        + short_taps[:, 2, None, :] * grad_ext[:, 2:]
    )
    return (mixed, stream_grads.astype(jnp.bfloat16))


def solution(mesh):
    return jax.shard_map(
        on_device,
        mesh=mesh,
        in_specs=(
            P(None, "seq", "tp"),
            P(None, None, "tp"),
            P("seq", "tp"),
            P("tp"),
            P("tp", None),
            P("seq", None),
        ),
        out_specs=(P("seq", "tp"), P(None, "seq", "tp")),
        check_vma=False,
    )
```

```python
import math

import jax
import jax.numpy as jnp
from jax import lax
from jax.sharding import PartitionSpec as P

full_turn = 2.0 * math.pi
fast = lax.Precision.HIGH


def passed_along(x, axis, by):
    devices = lax.axis_size(axis)
    pairs = [(i, i + by) for i in range(devices) if 0 <= i + by < devices]
    return lax.ppermute(x, axis, pairs)


def angle_table(rows, cols, period):
    row_ids = jnp.arange(rows, dtype=jnp.int32)[:, None]
    col_ids = jnp.arange(cols, dtype=jnp.int32)[None, :]
    angles = (row_ids * col_ids % period).astype(jnp.float32) * (full_turn / period)
    return (jnp.cos(angles), jnp.sin(angles))


def forward_spectra(lanes, total):
    count = lanes.shape[2]
    length = lanes.shape[1]
    half = count + 1
    cosine, sine = angle_table(half, count, 2 * count)
    first = jnp.einsum("rkm,simc->rsikc", jnp.stack([cosine, -sine]), lanes, precision=fast)
    twist_cos, twist_sin = angle_table(length, half, total)
    twist_cos = twist_cos[:, :, None]
    twist_sin = twist_sin[:, :, None]
    real_part = first[0] * twist_cos + first[1] * twist_sin
    imag_part = first[1] * twist_cos - first[0] * twist_sin
    cos_b, sin_b = angle_table(length, length, length)
    table = jnp.stack([cos_b - sin_b, cos_b, -sin_b])
    parts = jnp.stack([real_part, imag_part - real_part, real_part + imag_part])
    products = jnp.einsum("pji,psikc->psjkc", table, parts, precision=fast)
    return jnp.stack([products[0] - products[2], products[0] + products[1]])


def inverse_signals(spectral, count, total):
    length = spectral.shape[2]
    half = spectral.shape[3]
    cos_b, sin_b = angle_table(length, length, length)
    table = jnp.stack([cos_b + sin_b, cos_b, sin_b])
    parts = jnp.stack([spectral[0], spectral[1] - spectral[0], spectral[0] + spectral[1]])
    products = jnp.einsum("pij,psjkc->psikc", table, parts, precision=fast)
    block = jnp.stack([products[0] - products[2], products[0] + products[1]])
    twist_cos, twist_sin = angle_table(length, half, total)
    twist_cos = twist_cos[:, :, None]
    twist_sin = twist_sin[:, :, None]
    real_part = block[0] * twist_cos - block[1] * twist_sin
    imag_part = block[0] * twist_sin + block[1] * twist_cos
    cosine, sine = angle_table(count, half, 2 * count)
    k_ids = jnp.arange(half, dtype=jnp.int32)[None, :]
    weight = jnp.where((k_ids == 0) | (k_ids == count), 1.0, 2.0) * (1.0 / total)
    last = jnp.stack([cosine * weight, -sine * weight])
    return jnp.einsum(
        "rmk,rsikc->simc", last, jnp.stack([real_part, imag_part]), precision=fast
    )


def on_device(streams, short_taps, filter_taps, skip_gain, w_out, cotangent):
    length = streams.shape[1]
    channels = streams.shape[2]
    devices = lax.axis_size("seq")
    groups = lax.axis_size("tp")
    total = 2 * length * devices
    lane_width = channels // devices
    features = w_out.shape[1] // groups
    me = lax.axis_index("tp")

    def exchanged(x, shift):
        return lax.ppermute(x, "tp", [(i, (i + shift) % groups) for i in range(groups)])

    core = lax.axis_index("seq") % 2
    half_width = features // 2
    own_block = lax.dynamic_slice_in_dim(w_out, me * features, features, axis=1)
    pieces = [
        lax.dynamic_slice_in_dim(w_out, ((me + shift) % groups) * features + core * half_width, half_width, axis=1)
        for shift in range(1, groups)
    ]

    previous = passed_along(streams[:, -2:, :], "seq", 1)
    extended = jnp.concatenate([previous, streams], axis=1).astype(jnp.float32)
    convolved = (
        short_taps[:, 0, None, :] * extended[:, 2:]
        + short_taps[:, 1, None, :] * extended[:, 1:-1]
        + short_taps[:, 2, None, :] * extended[:, :-2]
    )
    conv_q = convolved[0]
    conv_k = convolved[1]
    conv_v = convolved[2]
    source = conv_k * conv_v
    grad_gated = lax.dot_general(
        cotangent, w_out, (((1,), (1,)), ((), ())), preferred_element_type=jnp.float32
    )
    grad_state = grad_gated * conv_q

    signals = jnp.stack([filter_taps, source, grad_state]).reshape(3, length, devices, lane_width)
    lanes = lax.all_to_all(signals, "seq", split_axis=2, concat_axis=2, tiled=True)
    fetched = jnp.stack([exchanged(piece, shift) for shift, piece in enumerate(pieces, 1)])
    partner = lax.ppermute(fetched, "seq", [(i, i ^ 1) for i in range(devices)])
    spectra = forward_spectra(lanes[:2], total)
    kernel_real = spectra[0, 0]
    kernel_imag = spectra[1, 0]
    data_real = spectra[0, 1]
    data_imag = spectra[1, 1]
    long_spectra = jnp.stack(
        [data_real * kernel_real - data_imag * kernel_imag, data_real * kernel_imag + data_imag * kernel_real]
    )[:, None]
    long_back = inverse_signals(long_spectra, devices, total)
    fetched, partner, long_back, grad_lanes = lax.optimization_barrier((fetched, partner, long_back, lanes[2:]))
    long_part = lax.all_to_all(long_back, "seq", split_axis=2, concat_axis=2, tiled=True)
    grad_spectra = forward_spectra(grad_lanes, total)
    grad_real = grad_spectra[0, 0]
    grad_imag = grad_spectra[1, 0]
    adjoint = jnp.stack(
        [grad_real * kernel_real + grad_imag * kernel_imag, grad_imag * kernel_real - grad_real * kernel_imag]
    )[:, None]
    grad_back = inverse_signals(adjoint, devices, total)

    mixer_state = long_part.reshape(length, channels) + skip_gain * source
    gated = (conv_q * mixer_state).astype(jnp.bfloat16)
    blocks = [own_block]
    for shift in range(1, groups):
        mine, other = fetched[shift - 1], partner[shift - 1]
        blocks.append(
            jnp.where(core == 0, jnp.concatenate([mine, other], axis=1), jnp.concatenate([other, mine], axis=1))
        )
    stacked = jnp.concatenate(blocks, axis=0)
    gated, stacked, grad_back = lax.optimization_barrier((gated, stacked, grad_back))
    grad_long = lax.all_to_all(grad_back, "seq", split_axis=2, concat_axis=2, tiled=True)
    gathered = jnp.concatenate([gated] + [exchanged(gated, shift) for shift in range(1, groups)], axis=1)
    terms = jnp.dot(gathered, stacked, preferred_element_type=jnp.float32)
    mixed = terms.astype(jnp.bfloat16)

    grad_q = grad_gated * mixer_state
    grad_source = grad_long.reshape(length, channels) + skip_gain * grad_state
    gradients = jnp.stack([grad_q, grad_source * conv_v, grad_source * conv_k])
    following = passed_along(gradients[:, :2, :], "seq", -1)
    grad_ext = jnp.concatenate([gradients, following], axis=1)
    stream_grads = (
        short_taps[:, 0, None, :] * grad_ext[:, :-2]
        + short_taps[:, 1, None, :] * grad_ext[:, 1:-1]
        + short_taps[:, 2, None, :] * grad_ext[:, 2:]
    )
    return (mixed, stream_grads.astype(jnp.bfloat16))


def solution(mesh):
    return jax.shard_map(
        on_device,
        mesh=mesh,
        in_specs=(
            P(None, "seq", "tp"),
            P(None, None, "tp"),
            P("seq", "tp"),
            P("tp"),
            P("tp", None),
            P("seq", None),
        ),
        out_specs=(P("seq", "tp"), P(None, "seq", "tp")),
        check_vma=False,
    )
```

```python
import math

import jax
import jax.numpy as jnp
from jax import lax
from jax.sharding import PartitionSpec as P

full_turn = 2.0 * math.pi
fast = lax.Precision.HIGH


def passed_along(x, axis, by):
    devices = lax.axis_size(axis)
    pairs = [(i, i + by) for i in range(devices) if 0 <= i + by < devices]
    return lax.ppermute(x, axis, pairs)


def angle_table(rows, cols, period):
    row_ids = jnp.arange(rows, dtype=jnp.int32)[:, None]
    col_ids = jnp.arange(cols, dtype=jnp.int32)[None, :]
    angles = (row_ids * col_ids % period).astype(jnp.float32) * (full_turn / period)
    return (jnp.cos(angles), jnp.sin(angles))


def forward_spectra(lanes, total):
    count = lanes.shape[2]
    length = lanes.shape[1]
    half = count + 1
    cosine, sine = angle_table(half, count, 2 * count)
    first = jnp.einsum("rkm,simc->rsikc", jnp.stack([cosine, -sine]), lanes, precision=fast)
    twist_cos, twist_sin = angle_table(length, half, total)
    twist_cos = twist_cos[:, :, None]
    twist_sin = twist_sin[:, :, None]
    real_part = first[0] * twist_cos + first[1] * twist_sin
    imag_part = first[1] * twist_cos - first[0] * twist_sin
    cos_b, sin_b = angle_table(length, length, length)
    table = jnp.stack([cos_b - sin_b, cos_b, -sin_b])
    parts = jnp.stack([real_part, imag_part - real_part, real_part + imag_part])
    products = jnp.einsum("pji,psikc->psjkc", table, parts, precision=fast)
    return jnp.stack([products[0] - products[2], products[0] + products[1]])


def inverse_signals(spectral, count, total):
    length = spectral.shape[2]
    half = spectral.shape[3]
    cos_b, sin_b = angle_table(length, length, length)
    table = jnp.stack([cos_b + sin_b, cos_b, sin_b])
    parts = jnp.stack([spectral[0], spectral[1] - spectral[0], spectral[0] + spectral[1]])
    products = jnp.einsum("pij,psjkc->psikc", table, parts, precision=fast)
    block = jnp.stack([products[0] - products[2], products[0] + products[1]])
    twist_cos, twist_sin = angle_table(length, half, total)
    twist_cos = twist_cos[:, :, None]
    twist_sin = twist_sin[:, :, None]
    real_part = block[0] * twist_cos - block[1] * twist_sin
    imag_part = block[0] * twist_sin + block[1] * twist_cos
    cosine, sine = angle_table(count, half, 2 * count)
    k_ids = jnp.arange(half, dtype=jnp.int32)[None, :]
    weight = jnp.where((k_ids == 0) | (k_ids == count), 1.0, 2.0) * (1.0 / total)
    last = jnp.stack([cosine * weight, -sine * weight])
    return jnp.einsum(
        "rmk,rsikc->simc", last, jnp.stack([real_part, imag_part]), precision=fast
    )


def on_device(streams, short_taps, filter_taps, skip_gain, w_out, cotangent):
    length = streams.shape[1]
    channels = streams.shape[2]
    devices = lax.axis_size("seq")
    groups = lax.axis_size("tp")
    total = 2 * length * devices
    lane_width = channels // devices
    features = w_out.shape[1] // groups
    me = lax.axis_index("tp")

    def exchanged(x, shift):
        return lax.ppermute(x, "tp", [(i, (i + shift) % groups) for i in range(groups)])

    core = lax.axis_index("seq") % 2
    half_width = features // 2
    own_block = lax.dynamic_slice_in_dim(w_out, me * features, features, axis=1)
    pieces = [
        lax.dynamic_slice_in_dim(w_out, ((me + shift) % groups) * features + core * half_width, half_width, axis=1)
        for shift in range(1, groups)
    ]

    previous = passed_along(streams[:, -2:, :], "seq", 1)
    extended = jnp.concatenate([previous, streams], axis=1).astype(jnp.float32)
    convolved = (
        short_taps[:, 0, None, :] * extended[:, 2:]
        + short_taps[:, 1, None, :] * extended[:, 1:-1]
        + short_taps[:, 2, None, :] * extended[:, :-2]
    )
    conv_q = convolved[0]
    conv_k = convolved[1]
    conv_v = convolved[2]
    source = conv_k * conv_v
    grad_gated = lax.dot_general(
        cotangent, w_out, (((1,), (1,)), ((), ())), preferred_element_type=jnp.float32
    )
    grad_state = grad_gated * conv_q

    signals = jnp.stack([filter_taps, source, grad_state]).reshape(3, length, devices, lane_width)
    lanes = lax.all_to_all(signals, "seq", split_axis=2, concat_axis=2, tiled=True)
    fetched = jnp.stack([exchanged(piece, shift) for shift, piece in enumerate(pieces, 1)])
    partner = lax.ppermute(fetched, "seq", [(i, i ^ 1) for i in range(devices)])
    spectra = forward_spectra(lanes, total)
    kernel_real = spectra[0, 0]
    kernel_imag = spectra[1, 0]
    data_real = spectra[0, 1]
    data_imag = spectra[1, 1]
    grad_real = spectra[0, 2]
    grad_imag = spectra[1, 2]
    long_spectra = jnp.stack(
        [data_real * kernel_real - data_imag * kernel_imag, data_real * kernel_imag + data_imag * kernel_real]
    )[:, None]
    long_back = inverse_signals(long_spectra, devices, total)
    fetched, partner, long_back = lax.optimization_barrier((fetched, partner, long_back))
    long_part = lax.all_to_all(long_back, "seq", split_axis=2, concat_axis=2, tiled=True)
    adjoint = jnp.stack(
        [grad_real * kernel_real + grad_imag * kernel_imag, grad_imag * kernel_real - grad_real * kernel_imag]
    )[:, None]
    grad_back = inverse_signals(adjoint, devices, total)

    mixer_state = long_part.reshape(length, channels) + skip_gain * source
    gated = (conv_q * mixer_state).astype(jnp.bfloat16)
    blocks = [own_block]
    for shift in range(1, groups):
        mine, other = fetched[shift - 1], partner[shift - 1]
        blocks.append(
            jnp.where(core == 0, jnp.concatenate([mine, other], axis=1), jnp.concatenate([other, mine], axis=1))
        )
    stacked = jnp.concatenate(blocks, axis=0)
    gated, stacked, grad_back = lax.optimization_barrier((gated, stacked, grad_back))
    grad_long = lax.all_to_all(grad_back, "seq", split_axis=2, concat_axis=2, tiled=True)
    own_terms = jnp.dot(gated, stacked[:channels], preferred_element_type=jnp.float32)
    gathered = jnp.concatenate([exchanged(gated, shift) for shift in range(1, groups)], axis=1)
    terms = own_terms + jnp.dot(gathered, stacked[channels:], preferred_element_type=jnp.float32)
    mixed = terms.astype(jnp.bfloat16)

    grad_q = grad_gated * mixer_state
    grad_source = grad_long.reshape(length, channels) + skip_gain * grad_state
    gradients = jnp.stack([grad_q, grad_source * conv_v, grad_source * conv_k])
    following = passed_along(gradients[:, :2, :], "seq", -1)
    grad_ext = jnp.concatenate([gradients, following], axis=1)
    stream_grads = (
        short_taps[:, 0, None, :] * grad_ext[:, :-2]
        + short_taps[:, 1, None, :] * grad_ext[:, 1:-1]
        + short_taps[:, 2, None, :] * grad_ext[:, 2:]
    )
    return (mixed, stream_grads.astype(jnp.bfloat16))


def solution(mesh):
    return jax.shard_map(
        on_device,
        mesh=mesh,
        in_specs=(
            P(None, "seq", "tp"),
            P(None, None, "tp"),
            P("seq", "tp"),
            P("tp"),
            P("tp", None),
            P("seq", None),
        ),
        out_specs=(P("seq", "tp"), P(None, "seq", "tp")),
        check_vma=False,
    )
```

```python
import math

import jax
import jax.numpy as jnp
from jax import lax
from jax.sharding import PartitionSpec as P

full_turn = 2.0 * math.pi
fast = lax.Precision.HIGH


def passed_along(x, axis, by):
    devices = lax.axis_size(axis)
    pairs = [(i, i + by) for i in range(devices) if 0 <= i + by < devices]
    return lax.ppermute(x, axis, pairs)


def angle_table(rows, cols, period):
    row_ids = jnp.arange(rows, dtype=jnp.int32)[:, None]
    col_ids = jnp.arange(cols, dtype=jnp.int32)[None, :]
    angles = (row_ids * col_ids % period).astype(jnp.float32) * (full_turn / period)
    return (jnp.cos(angles), jnp.sin(angles))


def forward_spectra(lanes, total):
    count = lanes.shape[2]
    length = lanes.shape[1]
    half = count + 1
    cosine, sine = angle_table(half, count, 2 * count)
    first = jnp.einsum("rkm,simc->rsikc", jnp.stack([cosine, -sine]), lanes, precision=fast)
    twist_cos, twist_sin = angle_table(length, half, total)
    twist_cos = twist_cos[:, :, None]
    twist_sin = twist_sin[:, :, None]
    real_part = first[0] * twist_cos + first[1] * twist_sin
    imag_part = first[1] * twist_cos - first[0] * twist_sin
    cos_b, sin_b = angle_table(length, length, length)
    table = jnp.stack([cos_b - sin_b, cos_b, -sin_b])
    parts = jnp.stack([real_part, imag_part - real_part, real_part + imag_part])
    products = jnp.einsum("pji,psikc->psjkc", table, parts, precision=fast)
    return jnp.stack([products[0] - products[2], products[0] + products[1]])


def inverse_signals(spectral, count, total):
    length = spectral.shape[2]
    half = spectral.shape[3]
    cos_b, sin_b = angle_table(length, length, length)
    table = jnp.stack([cos_b + sin_b, cos_b, sin_b])
    parts = jnp.stack([spectral[0], spectral[1] - spectral[0], spectral[0] + spectral[1]])
    products = jnp.einsum("pij,psjkc->psikc", table, parts, precision=fast)
    block = jnp.stack([products[0] - products[2], products[0] + products[1]])
    twist_cos, twist_sin = angle_table(length, half, total)
    twist_cos = twist_cos[:, :, None]
    twist_sin = twist_sin[:, :, None]
    real_part = block[0] * twist_cos - block[1] * twist_sin
    imag_part = block[0] * twist_sin + block[1] * twist_cos
    cosine, sine = angle_table(count, half, 2 * count)
    k_ids = jnp.arange(half, dtype=jnp.int32)[None, :]
    weight = jnp.where((k_ids == 0) | (k_ids == count), 1.0, 2.0) * (1.0 / total)
    last = jnp.stack([cosine * weight, -sine * weight])
    return jnp.einsum(
        "rmk,rsikc->simc", last, jnp.stack([real_part, imag_part]), precision=fast
    )


def on_device(streams, short_taps, filter_taps, skip_gain, w_out, cotangent):
    length = streams.shape[1]
    channels = streams.shape[2]
    devices = lax.axis_size("seq")
    groups = lax.axis_size("tp")
    total = 2 * length * devices
    lane_width = channels // devices
    features = w_out.shape[1] // groups
    me = lax.axis_index("tp")

    def exchanged(x, shift):
        return lax.ppermute(x, "tp", [(i, (i + shift) % groups) for i in range(groups)])

    core = lax.axis_index("seq") % 2
    half_width = features // 2
    own_block = lax.dynamic_slice_in_dim(w_out, me * features, features, axis=1)
    pieces = [
        lax.dynamic_slice_in_dim(w_out, ((me + shift) % groups) * features + core * half_width, half_width, axis=1)
        for shift in range(1, groups)
    ]

    previous = passed_along(streams[:, -2:, :], "seq", 1)
    extended = jnp.concatenate([previous, streams], axis=1).astype(jnp.float32)
    convolved = (
        short_taps[:, 0, None, :] * extended[:, 2:]
        + short_taps[:, 1, None, :] * extended[:, 1:-1]
        + short_taps[:, 2, None, :] * extended[:, :-2]
    )
    conv_q = convolved[0]
    conv_k = convolved[1]
    conv_v = convolved[2]
    source = conv_k * conv_v
    grad_gated = lax.dot_general(
        cotangent, w_out, (((1,), (1,)), ((), ())), preferred_element_type=jnp.float32
    )
    grad_state = grad_gated * conv_q

    signals = jnp.stack([filter_taps, source, grad_state]).reshape(3, length, devices, lane_width)
    lanes = lax.all_to_all(signals, "seq", split_axis=2, concat_axis=2, tiled=True)
    fetched = jnp.stack([exchanged(piece, shift) for shift, piece in enumerate(pieces, 1)])
    partner = lax.ppermute(fetched, "seq", [(i, i ^ 1) for i in range(devices)])
    spectra = forward_spectra(lanes, total)
    kernel_real = spectra[0, 0]
    kernel_imag = spectra[1, 0]
    data_real = spectra[0, 1]
    data_imag = spectra[1, 1]
    grad_real = spectra[0, 2]
    grad_imag = spectra[1, 2]
    long_spectra = jnp.stack(
        [data_real * kernel_real - data_imag * kernel_imag, data_real * kernel_imag + data_imag * kernel_real]
    )[:, None]
    long_back = inverse_signals(long_spectra, devices, total)
    fetched, partner, long_back = lax.optimization_barrier((fetched, partner, long_back))
    long_part = lax.all_to_all(long_back, "seq", split_axis=2, concat_axis=2, tiled=True)
    adjoint = jnp.stack(
        [grad_real * kernel_real + grad_imag * kernel_imag, grad_imag * kernel_real - grad_real * kernel_imag]
    )[:, None]
    grad_back = inverse_signals(adjoint, devices, total)

    mixer_state = long_part.reshape(length, channels) + skip_gain * source
    gated = (conv_q * mixer_state).astype(jnp.bfloat16)
    blocks = [own_block]
    for shift in range(1, groups):
        mine, other = fetched[shift - 1], partner[shift - 1]
        blocks.append(
            jnp.where(core == 0, jnp.concatenate([mine, other], axis=1), jnp.concatenate([other, mine], axis=1))
        )
    stacked = jnp.concatenate(blocks, axis=0)
    gated, stacked, grad_back = lax.optimization_barrier((gated, stacked, grad_back))
    grad_long = lax.all_to_all(grad_back, "seq", split_axis=2, concat_axis=2, tiled=True)
    own_terms = jnp.dot(gated, stacked[:channels], preferred_element_type=jnp.float32)
    gathered = jnp.concatenate([exchanged(gated, shift) for shift in range(1, groups)], axis=1)
    terms = own_terms + jnp.dot(gathered, stacked[channels:], preferred_element_type=jnp.float32)
    mixed = terms.astype(jnp.bfloat16)

    def ahead(gradients, taps):
        following = passed_along(gradients[:, :2, :], "seq", -1)
        grad_ext = jnp.concatenate([gradients, following], axis=1)
        return (
            taps[:, 0, None, :] * grad_ext[:, :-2]
            + taps[:, 1, None, :] * grad_ext[:, 1:-1]
            + taps[:, 2, None, :] * grad_ext[:, 2:]
        )

    grad_q = grad_gated * mixer_state
    q_grads = ahead(grad_q[None], short_taps[:1])
    grad_source = grad_long.reshape(length, channels) + skip_gain * grad_state
    kv_grads = ahead(jnp.stack([grad_source * conv_v, grad_source * conv_k]), short_taps[1:])
    stream_grads = jnp.concatenate([q_grads, kv_grads], axis=0)
    return (mixed, stream_grads.astype(jnp.bfloat16))


def solution(mesh):
    return jax.shard_map(
        on_device,
        mesh=mesh,
        in_specs=(
            P(None, "seq", "tp"),
            P(None, None, "tp"),
            P("seq", "tp"),
            P("tp"),
            P("tp", None),
            P("seq", None),
        ),
        out_specs=(P("seq", "tp"), P(None, "seq", "tp")),
        check_vma=False,
    )
```
